512 devices in a mesh: dp: 8 (over y_lo, core), seq: 64 (over x, z, y_hi).
Axes of the slice: x: 4, y: 8 (y_hi: 2, y_lo: 4; y = y_hi * 4 + y_lo), z: 8, core: 2. Of those that a mesh axis runs over, the one named last changes fastest.
Arguments:
- queries: bfloat16 [8, 8192, 2048], P('dp', 'seq'), may hold values from -62 to 62
- keys: bfloat16 [8, 8192, 2048], P('dp', 'seq'), may hold values from -4 to 4
- values: bfloat16 [8, 8192, 2048], P('dp', 'seq'), may hold values from -4 to 4
- cotangent: bfloat16 [8, 8192, 2048], P('dp', 'seq'), may hold values from -4 to 4
- cluster_of: int32 [8, 16, 128], P('dp', None, 'seq'), may hold values from 0 to 127, as said below
- block_list: int32 [8, 2048, 4], P('dp', 'seq'), may hold values from -1 to 127, as said below
- centroid_sums: float32 [2048, 128], P('seq'), may hold values from -5 to 5
Outputs:
- attn_out: bfloat16 [8, 8192, 2048], P('dp', 'seq')
- grad_q: bfloat16 [8, 8192, 2048], P('dp', 'seq')
- grad_k: bfloat16 [8, 8192, 2048], P('dp', 'seq')
- grad_v: bfloat16 [8, 8192, 2048], P('dp', 'seq')
- centroid_next: float32 [2048, 128], P('seq')
The draws below stay inside these ranges and needn't reach their ends.
Inputs may be any that keep to these rules, and one draw needn't show every extreme that they name: cluster_of[d, h, b] is the cluster under head h of block b of document d; the centroid of cluster c of head h lies on seq index h * 4 + c // 32. Of the 2 blocks on one seq index, at most 1 share the value c // 32 under one head, and in every draw some reach 1. Row h * 128 + c of block_list[d] lists in increasing order the blocks b with cluster_of[d, h, b] == c, then -1; every block appears once for each head; a cluster holds at most 4 blocks, and in every draw some cluster holds exactly 4.
All inputs are finite; a program needn't handle non-finite values.
Results may differ from the reference program's by a relative error of at most 0.015.
Values may be sent and summed in bfloat16 or wider, within the bound.
No kernel may reach another device: no remote copies, remote signals or barrier semaphores. Data moves between devices by JAX's collectives and lax.ppermute only.
A program may use at most 64 MiB of HBM per device.

```python
import math
import jax
import jax.numpy as jnp
from jax import lax

HEADS = 16
HD = 128
CENT = 128
BLK = 64
DOCS = 8
TOKENS = 8192
BLOCKS = 128
BLK_DEV = 2
OWN_H = 4
CL_DEV = 32
CAP = 1
MOST = 4
N_SEQ = 64


def route_tables(base_key):
    key_owner = jax.random.fold_in(base_key, 701)
    key_forced = jax.random.fold_in(base_key, 702)
    key_first = jax.random.fold_in(base_key, 703)
    key_order = jax.random.fold_in(base_key, 704)
    key_full = jax.random.fold_in(base_key, 705)
    key_slots = jax.random.fold_in(base_key, 706)
    owner_keys = jax.random.split(key_owner, DOCS * HEADS * N_SEQ)
    drawn = jax.vmap(lambda single: jax.random.permutation(single, OWN_H * CAP)[:BLK_DEV])(owner_keys)
    owner_local = (drawn // CAP).astype(jnp.int32).reshape(DOCS, HEADS, N_SEQ, BLK_DEV)
    forced_owner = jax.random.randint(key_forced, (DOCS, HEADS, 1, 1), 0, OWN_H)
    first_device = jax.random.randint(key_first, (DOCS, HEADS, 1), 0, N_SEQ)
    device_ids = jnp.arange(N_SEQ, dtype=jnp.int32)[None, None, :]
    forced_device = (device_ids - first_device) % N_SEQ < MOST
    rotated = (jnp.arange(BLK_DEV, dtype=jnp.int32)[None, None, None, :] // CAP + forced_owner) % OWN_H
    owner_local = jnp.where(forced_device[..., None], rotated, owner_local).reshape(DOCS, HEADS, BLOCKS)
    block_first = (jnp.arange(BLK_DEV, dtype=jnp.int32) == 0)[None, None, None, :]
    forced_block = (forced_device[..., None] & block_first).reshape(DOCS, HEADS, BLOCKS)
    order_key = jax.random.randint(key_order, (DOCS, HEADS, BLOCKS), 0, 1 << 20)
    order_key = jnp.where(forced_block, 0, order_key + 1)
    block_ids = jnp.arange(BLOCKS, dtype=jnp.int32)

    def rank_one(packed):
        owners, order_row = packed
        same_owner = owners[None, :] == owners[:, None]
        earlier = (order_row[None, :] < order_row[:, None]) | (order_row[None, :] == order_row[:, None]) & (block_ids[None, :] < block_ids[:, None])
        return jnp.sum(same_owner & earlier, axis=1).astype(jnp.int32)
    rank_at = lax.map(rank_one, (owner_local.reshape(-1, BLOCKS), order_key.reshape(-1, BLOCKS))).reshape(DOCS, HEADS, BLOCKS)
    full_cluster = jax.random.randint(key_full, (DOCS, HEADS, OWN_H), 0, CL_DEV)
    spare_slots = (CL_DEV - 1) * MOST
    slot_keys = jax.random.split(key_slots, DOCS * HEADS * OWN_H)
    spare_order = jax.vmap(lambda single: jax.random.permutation(single, spare_slots))(slot_keys).astype(jnp.int32)
    spare_order = spare_order.reshape(DOCS, HEADS, OWN_H * spare_slots)
    full_block = jnp.take_along_axis(full_cluster, owner_local, axis=2)
    slot_index = jnp.clip(rank_at - MOST, 0, spare_slots - 1)
    chosen = jnp.take_along_axis(spare_order, owner_local * spare_slots + slot_index, axis=2)
    spare_cluster = chosen // MOST
    spare_cluster = spare_cluster + (spare_cluster >= full_block).astype(jnp.int32)
    local_cluster = jnp.where(rank_at < MOST, full_block, spare_cluster)
    cluster_ids = (owner_local * CL_DEV + local_cluster).astype(jnp.int32)

    def list_one(cluster_row):
        same_cluster = cluster_row[None, :] == cluster_row[:, None]
        position = jnp.sum(same_cluster & (block_ids[None, :] < block_ids[:, None]), axis=1).astype(jnp.int32)
        return jnp.full((CENT, MOST), -1, jnp.int32).at[cluster_row, position].set(block_ids)
    block_lists = lax.map(list_one, cluster_ids.reshape(-1, BLOCKS)).reshape(DOCS, HEADS * CENT, MOST)
    return (cluster_ids, block_lists)


def draw_cluster_of(key, part):
    return route_tables(key)[0]


def draw_block_list(key, part):
    return route_tables(key)[1]


def query_key_pair(base_key):
    key_query = jax.random.fold_in(base_key, 901)
    key_keys = jax.random.fold_in(base_key, 902)
    shape_all = (DOCS, TOKENS, HEADS * HD)
    keys_out = jnp.clip(jax.random.normal(key_keys, shape_all, jnp.float32), -4.0, 4.0)
    queries_out = jnp.clip(jax.random.normal(key_query, shape_all, jnp.float32), -4.0, 4.0)
    return (queries_out, keys_out)


def draw_queries(key, part):
    return query_key_pair(key)[0].astype(jnp.bfloat16)


def draw_keys(key, part):
    return query_key_pair(key)[1].astype(jnp.bfloat16)


def level_of(own_key, extent, shards, least, largest):
    def one(axis_at, parts):
        steps = jax.random.uniform(jax.random.fold_in(jax.random.fold_in(own_key, 6), axis_at), (parts,), jnp.float32, least / len(shards), largest / len(shards))
        return jnp.repeat(jnp.exp(steps), extent[axis_at] // parts).reshape((-1,) + (1,) * (len(extent) - axis_at - 1))

    gain = one(*shards[0])
    for cut in shards[1:]:
        gain = gain * one(*cut)
    return gain


def noise(stream_key, shape, scale, limit, cuts=(), held_as=jnp.bfloat16):
    loudness = level_of(stream_key, shape, cuts, -0.22, 0.18) if cuts else 1.0
    result = jax.random.normal(stream_key, shape, jnp.float32) * scale * loudness
    return jnp.minimum(jnp.maximum(result, -limit), limit).astype(held_as)


def setup_inputs(seed: int = 0) -> dict:
    key_of = jax.random.split(jax.random.key(seed), 8)
    return {
        "queries": draw_queries(jax.random.fold_in(key_of[7], 71), 0),
        "keys": draw_keys(jax.random.fold_in(key_of[7], 71), 0),
        "values": noise(key_of[2], (DOCS, TOKENS, HEADS * HD), 1.0, 4.0, ((0, 8), (1, 64))),
        "cotangent": noise(key_of[3], (DOCS, TOKENS, HEADS * HD), 1.0, 4.0, ((0, 8), (1, 64))),
        "cluster_of": draw_cluster_of(jax.random.fold_in(key_of[7], 71), 0),
        "block_list": draw_block_list(jax.random.fold_in(key_of[7], 71), 0),
        "centroid_sums": noise(key_of[6], (HEADS * CENT, HD), 1.0, 5.0, ((0, 64),), jnp.float32),
    }


decay_rate = 0.99
neg_fill = -1e+30

def attend(q_tiles, k_tiles, v_tiles, d_tiles, positions, present_rows, cluster_rows):
    score_scale = 1.0 / math.sqrt(q_tiles.shape[-1])
    q_wide = q_tiles.astype(jnp.float32)
    k_wide = k_tiles.astype(jnp.float32)
    v_wide = v_tiles.astype(jnp.float32)
    d_wide = d_tiles.astype(jnp.float32)
    scores = jnp.einsum('crd,csd->crs', q_wide, k_wide) * score_scale
    visible = present_rows[:, :, None] & present_rows[:, None, :]
    visible = visible & (positions[:, None, :] <= positions[:, :, None])
    visible = visible & (cluster_rows[:, None, :] == cluster_rows[:, :, None])
    scores = jnp.where(visible, scores, neg_fill)
    row_max = lax.optimization_barrier(jnp.max(scores, axis=-1, keepdims=True))
    raised = jnp.exp(scores - row_max)
    probabilities = jnp.where(visible, raised / lax.optimization_barrier(jnp.sum(raised, axis=-1, keepdims=True)), 0.0)
    weights = lax.optimization_barrier(probabilities.astype(jnp.bfloat16)).astype(jnp.float32)
    out_full = jnp.einsum('crs,csd->crd', weights, v_wide)
    dprobs = jnp.einsum('crd,csd->crs', d_wide, v_wide)
    row_dot = lax.optimization_barrier(jnp.sum(d_wide * out_full, axis=-1, keepdims=True))
    dscores = (probabilities * (dprobs - row_dot) * score_scale).astype(jnp.bfloat16)
    dscores = lax.optimization_barrier(dscores).astype(jnp.float32)
    grad_values = jnp.einsum('crs,crd->csd', weights, d_wide)
    grad_queries = jnp.einsum('crs,csd->crd', dscores, k_wide)
    grad_keys = jnp.einsum('crs,crd->csd', dscores, q_wide)
    return (out_full, grad_queries, grad_keys, grad_values)

def one_head(packed):
    q_head, k_head, v_head, d_head, cluster_row, lists_head = packed
    members = lists_head.reshape(-1)
    present = members >= 0
    picked = jnp.where(present, members, 0).astype(jnp.int32)
    token_offsets = jnp.arange(BLK, dtype=jnp.int32)
    positions = (picked[:, None] * BLK + token_offsets[None, :]).reshape(CENT, MOST * BLK)
    present_rows = jnp.broadcast_to(present[:, None], (CENT * MOST, BLK)).reshape(CENT, MOST * BLK)
    block_cluster = cluster_row[picked]
    cluster_rows = jnp.broadcast_to(block_cluster[:, None], (CENT * MOST, BLK)).reshape(CENT, MOST * BLK)

    def gather_tiles(source):
        return source.reshape(BLOCKS, BLK, HD)[picked].reshape(CENT, MOST * BLK, HD)
    k_tiles = gather_tiles(k_head)
    results = attend(gather_tiles(q_head), k_tiles, gather_tiles(v_head), gather_tiles(d_head), positions, present_rows, cluster_rows)
    key_sum = lax.optimization_barrier(jnp.sum(jnp.where(present_rows[:, :, None], k_tiles.astype(jnp.float32), 0.0), axis=1))
    target = jnp.where(present, members, BLOCKS).astype(jnp.int32)

    def scatter_tiles(tiles_in):
        placed = jnp.zeros((BLOCKS, BLK, HD), jnp.bfloat16)
        placed = placed.at[target].set(tiles_in.astype(jnp.bfloat16).reshape(CENT * MOST, BLK, HD), mode='drop')
        return placed.reshape(TOKENS, HD)
    return (scatter_tiles(results[0]), scatter_tiles(results[1]), scatter_tiles(results[2]), scatter_tiles(results[3]), key_sum)

def reference(queries, keys, values, cotangent, cluster_of, block_list, centroid_sums):

    def split_heads(source):
        return source.reshape(DOCS, TOKENS, HEADS, HD).transpose(0, 2, 1, 3).reshape(DOCS * HEADS, TOKENS, HD)

    def join_heads(source):
        return source.reshape(DOCS, HEADS, TOKENS, HD).transpose(0, 2, 1, 3).reshape(DOCS, TOKENS, HEADS * HD)
    lists_all = block_list.reshape(DOCS * HEADS, CENT, MOST)
    clusters_all = cluster_of.reshape(DOCS * HEADS, BLOCKS)
    results = lax.map(one_head, (split_heads(queries), split_heads(keys), split_heads(values), split_heads(cotangent), clusters_all, lists_all))
    key_sum = lax.optimization_barrier(jnp.sum(results[4].reshape(DOCS, HEADS * CENT, HD), axis=0))
    centroid_next = decay_rate * centroid_sums + (1.0 - decay_rate) * key_sum
    return (join_heads(results[0]), join_heads(results[1]), join_heads(results[2]), join_heads(results[3]), centroid_next)
```

```python
import math

import jax
import jax.numpy as jnp
from jax import lax
from jax.sharding import PartitionSpec as P

decay_rate = 0.99
neg_fill = -1e30


def shortened(x):
    return jax.tree.map(lambda a: a.astype(jnp.bfloat16) if a.dtype == jnp.float32 else a, x)


def forward_tiles(q_tiles, k_tiles, v_tiles, positions, present_rows):
    score_scale = 1.0 / math.sqrt(q_tiles.shape[-1])
    scores = (
        jnp.einsum("crd,csd->crs", q_tiles, k_tiles, preferred_element_type=jnp.float32)
        * score_scale
    )
    visible = present_rows[:, :, None] & present_rows[:, None, :]
    visible = visible & (positions[:, None, :] <= positions[:, :, None])
    scores = jnp.where(visible, scores, neg_fill)
    row_max = jnp.max(scores, axis=-1, keepdims=True)
    raised = jnp.exp(scores - row_max)
    probabilities = jnp.where(visible, raised / jnp.sum(raised, axis=-1, keepdims=True), 0.0)
    weights = probabilities.astype(jnp.bfloat16)
    out_full = jnp.einsum("crs,csd->crd", weights, v_tiles, preferred_element_type=jnp.float32)
    return (probabilities, weights, out_full, score_scale)


def output_tiles(q_tiles, k_tiles, v_tiles, positions, present_rows):
    results = forward_tiles(q_tiles, k_tiles, v_tiles, positions, present_rows)
    return (results[2].astype(jnp.bfloat16),)


def all_tiles(q_tiles, k_tiles, v_tiles, d_tiles, positions, present_rows):
    probabilities, weights, out_full, score_scale = forward_tiles(
        q_tiles, k_tiles, v_tiles, positions, present_rows
    )
    dprobs = jnp.einsum("crd,csd->crs", d_tiles, v_tiles, preferred_element_type=jnp.float32)
    row_dot = jnp.sum(d_tiles.astype(jnp.float32) * out_full, axis=-1, keepdims=True)
    dscores = (probabilities * (dprobs - row_dot) * score_scale).astype(jnp.bfloat16)
    grad_values = jnp.einsum("crs,crd->csd", weights, d_tiles, preferred_element_type=jnp.float32)
    grad_queries = jnp.einsum("crs,csd->crd", dscores, k_tiles, preferred_element_type=jnp.float32)
    grad_keys = jnp.einsum("crs,crd->csd", dscores, q_tiles, preferred_element_type=jnp.float32)
    return (
        out_full.astype(jnp.bfloat16),
        grad_queries.astype(jnp.bfloat16),
        grad_keys.astype(jnp.bfloat16),
        grad_values.astype(jnp.bfloat16),
    )


def grad_tiles(q_tiles, k_tiles, v_tiles, d_tiles, positions, present_rows):
    return all_tiles(q_tiles, k_tiles, v_tiles, d_tiles, positions, present_rows)[1:]


def per_device(queries, keys, values, cotangent, cluster_of, block_list, centroid_sums):
    seq_size = lax.axis_size("seq")
    head_count = cluster_of.shape[1]
    block_count = cluster_of.shape[2]
    token_count = queries.shape[1]
    block_len = token_count // block_count
    head_dim = centroid_sums.shape[1]
    groups_here = block_list.shape[1]
    cluster_cap = block_list.shape[2]
    owner_count = seq_size // head_count
    slot_cap = min(block_count, max(1, 2 * block_count // owner_count))
    tile_rows = cluster_cap * block_len
    step_target = 1 << max(0, max(1, 2048 // tile_rows).bit_length() - 1)
    group_size = math.gcd(groups_here, step_target)
    cluster_ids = cluster_of[0]
    owner_local = cluster_ids // groups_here
    earlier = jnp.arange(block_count)[:, None] < jnp.arange(block_count)[None, :]
    same_owner = owner_local[:, :, None] == owner_local[:, None, :]
    slot_of = jnp.sum(same_owner & earlier[None], axis=1)
    selector = owner_local[:, None, None, :] == jnp.arange(owner_count)[None, :, None, None]
    selector = selector & (slot_of[:, None, None, :] == jnp.arange(slot_cap)[None, None, :, None])
    selector = selector.astype(jnp.bfloat16)

    def pack(sources):
        stacked = jnp.stack([item[0] for item in sources])
        blocks_in = stacked.reshape(len(sources), block_count, block_len, head_count, head_dim)
        outgoing = jnp.einsum(
            "hlcj,ajthd->hlcatd", selector, blocks_in, preferred_element_type=jnp.float32
        )
        return outgoing.astype(jnp.bfloat16).reshape(
            seq_size * slot_cap, len(sources), block_len, head_dim
        )

    def unpack(returned):
        count = returned.shape[0]
        arranged = returned.reshape(count, head_count, owner_count, slot_cap, block_len, head_dim)
        gathered = jnp.einsum(
            "hlcj,ahlctd->ajthd", selector, arranged, preferred_element_type=jnp.float32
        )
        gathered = gathered.astype(jnp.bfloat16).reshape(count, 1, token_count, head_count * head_dim)
        return tuple(gathered[index] for index in range(count))

    members = block_list[0].reshape(-1)
    present = members >= 0
    source_dev = jnp.where(present, members // block_count, -1)
    before = (
        present[None, :]
        & (source_dev[None, :] == source_dev[:, None])
        & (members[None, :] < members[:, None])
    )
    slot_at = jnp.sum(before, axis=1)
    recv_row = jnp.where(present, source_dev * slot_cap + slot_at, 0)
    slot_ids = jnp.arange(seq_size * slot_cap)
    hit = present[None, :] & (recv_row[None, :] == slot_ids[:, None])
    member_of_slot = jnp.sum(jnp.where(hit, jnp.arange(members.shape[0])[None, :], 0), axis=1)
    slot_used = jnp.any(hit, axis=1)
    token_offsets = jnp.arange(block_len)
    positions = (
        jnp.where(present, members, 0)[:, None] * block_len + token_offsets[None, :]
    ).reshape(groups_here, tile_rows)
    present_rows = jnp.broadcast_to(present[:, None], (members.shape[0], block_len)).reshape(
        groups_here, tile_rows
    )

    def grouped(worker, tiles_all):
        shaped = tuple(
            (
                item.reshape((groups_here // group_size, group_size) + item.shape[1:])
                for item in tiles_all
            )
        )
        outcome = lax.map(lambda tiles_in: worker(*tiles_in), shaped)
        return tuple((item.reshape((groups_here,) + item.shape[2:]) for item in outcome))

    arrived = lax.all_to_all(
        pack((queries, keys, values, cotangent)), "seq", split_axis=0, concat_axis=0, tiled=True
    )
    picked = arrived[recv_row]
    q_tiles, key_tiles, v_tiles, d_tiles = (
        picked[:, index].reshape(groups_here, tile_rows, head_dim) for index in range(4)
    )
    key_sum = jnp.einsum(
        "cr,crd->cd",
        present_rows.astype(jnp.bfloat16),
        key_tiles,
        preferred_element_type=jnp.float32,
    )
    summed = jnp.sum(lax.all_gather(key_sum, "dp"), axis=0)
    results = grouped(all_tiles, (q_tiles, key_tiles, v_tiles, d_tiles, positions, present_rows))
    by_member = jnp.stack(
        [item.reshape(groups_here * cluster_cap, block_len, head_dim) for item in results]
    )
    outgoing = jnp.where(
        slot_used[None, :, None, None], by_member[:, member_of_slot], jnp.zeros((), jnp.bfloat16)
    )
    returned = lax.all_to_all(outgoing, "seq", split_axis=1, concat_axis=1, tiled=True)
    centroid_next = decay_rate * centroid_sums + (1.0 - decay_rate) * summed
    return unpack(returned) + (centroid_next,)


def solution(mesh):
    in_specs = (
        P("dp", "seq", None),
        P("dp", "seq", None),
        P("dp", "seq", None),
        P("dp", "seq", None),
        P("dp", None, "seq"),
        P("dp", "seq", None),
        P("seq", None),
    )
    out_specs = (
        P("dp", "seq", None),
        P("dp", "seq", None),
        P("dp", "seq", None),
        P("dp", "seq", None),
        P("seq", None),
    )
    return jax.shard_map(
        per_device, mesh=mesh, in_specs=in_specs, out_specs=out_specs, check_vma=False
    )
```

```python
import math

import jax
import jax.numpy as jnp
from jax import lax
from jax.experimental import pallas as pl
from jax.experimental.pallas import tpu as pltpu
from jax.sharding import PartitionSpec as P

decay_rate = 0.99
neg_fill = -1e30


def attend_block(q, k, v, g, query_pos, key_pos):
    score_scale = 1.0 / math.sqrt(q.shape[-1])
    scores = (
        lax.dot_general(q, k, (((1,), (1,)), ((), ())), preferred_element_type=jnp.float32)
        * score_scale
    )
    visible = key_pos <= query_pos
    scores = jnp.where(visible, scores, neg_fill)
    row_max = jnp.max(scores, axis=-1, keepdims=True)
    raised = jnp.exp(scores - row_max)
    probabilities = jnp.where(visible, raised / jnp.sum(raised, axis=-1, keepdims=True), 0.0)
    weights = probabilities.astype(jnp.bfloat16)
    out_full = jnp.dot(weights, v, preferred_element_type=jnp.float32)
    dprobs = lax.dot_general(g, v, (((1,), (1,)), ((), ())), preferred_element_type=jnp.float32)
    row_dot = jnp.sum(g.astype(jnp.float32) * out_full, axis=-1, keepdims=True)
    dscores_wide = probabilities * (dprobs - row_dot) * score_scale
    dscores = dscores_wide.astype(jnp.bfloat16)
    grad_values = jnp.dot(
        probabilities.T.astype(jnp.bfloat16), g, preferred_element_type=jnp.float32
    )
    grad_queries = jnp.dot(dscores, k, preferred_element_type=jnp.float32)
    grad_keys = jnp.dot(dscores_wide.T.astype(jnp.bfloat16), q, preferred_element_type=jnp.float32)
    return (out_full, grad_queries, grad_keys, grad_values)


def routed_kernel(recv_ref, count_ref, member_ref, arrived_ref, out_ref):
    cluster_count, cluster_cap = member_ref.shape
    block_len = arrived_ref.shape[2]
    out_ref[...] = jnp.zeros(out_ref.shape, out_ref.dtype)

    def one_cluster(cluster, carry):
        present_count = count_ref[cluster]
        for used in range(1, cluster_cap + 1):

            @pl.when(present_count == used)
            def _():
                rows = [recv_ref[cluster, slot] for slot in range(used)]
                tiles = [
                    jnp.concatenate([arrived_ref[row, index] for row in rows], axis=0)
                    for index in range(4)
                ]
                offsets = lax.broadcasted_iota(jnp.int32, (used * block_len, 1), 0)
                query_pos = offsets % block_len
                key_offsets = lax.broadcasted_iota(jnp.int32, (1, used * block_len), 1)
                key_pos = key_offsets % block_len
                for slot in range(used):
                    base = member_ref[cluster, slot] * block_len
                    query_pos = jnp.where(offsets // block_len == slot, query_pos + base, query_pos)
                    key_pos = jnp.where(key_offsets // block_len == slot, key_pos + base, key_pos)
                results = attend_block(*tiles, query_pos, key_pos)
                for slot in range(used):
                    for index in range(4):
                        out_ref[rows[slot], index] = results[index][
                            slot * block_len : (slot + 1) * block_len
                        ].astype(out_ref.dtype)

        return carry

    lax.fori_loop(0, cluster_count, one_cluster, 0)


def routed_attention(recv_table, present_count, member_table, arrived):
    smem = pl.BlockSpec(memory_space=pltpu.SMEM)
    vmem = pl.BlockSpec(memory_space=pltpu.VMEM)
    return pl.pallas_call(
        routed_kernel,
        out_shape=jax.ShapeDtypeStruct(arrived.shape, arrived.dtype),
        in_specs=[smem, smem, smem, vmem],
        out_specs=vmem,
    )(recv_table, present_count, member_table, arrived)


def per_device(queries, keys, values, cotangent, cluster_of, block_list, centroid_sums):
    seq_size = lax.axis_size("seq")
    head_count = cluster_of.shape[1]
    block_count = cluster_of.shape[2]
    token_count = queries.shape[1]
    block_len = token_count // block_count
    head_dim = centroid_sums.shape[1]
    groups_here = block_list.shape[1]
    cluster_cap = block_list.shape[2]
    owner_count = seq_size // head_count
    slot_cap = min(block_count, max(1, 2 * block_count // owner_count))
    cluster_ids = cluster_of[0]
    owner_local = cluster_ids // groups_here
    earlier = jnp.arange(block_count)[:, None] < jnp.arange(block_count)[None, :]
    same_owner = owner_local[:, :, None] == owner_local[:, None, :]
    slot_of = jnp.sum(same_owner & earlier[None], axis=1)
    selector = owner_local[:, None, None, :] == jnp.arange(owner_count)[None, :, None, None]
    selector = selector & (slot_of[:, None, None, :] == jnp.arange(slot_cap)[None, None, :, None])
    selector = selector.astype(jnp.bfloat16)

    def pack(sources):
        stacked = jnp.stack([item[0] for item in sources])
        blocks_in = stacked.reshape(len(sources), block_count, block_len, head_count, head_dim)
        outgoing = jnp.einsum(
            "hlcj,ajthd->hlcatd", selector, blocks_in, preferred_element_type=jnp.float32
        )
        return outgoing.astype(jnp.bfloat16).reshape(
            seq_size * slot_cap, len(sources), block_len, head_dim
        )

    def unpack(returned):
        count = returned.shape[1]
        arranged = returned.reshape(head_count, owner_count, slot_cap, count, block_len, head_dim)
        gathered = jnp.einsum(
            "hlcj,hlcatd->ajthd", selector, arranged, preferred_element_type=jnp.float32
        )
        gathered = gathered.astype(jnp.bfloat16).reshape(count, 1, token_count, head_count * head_dim)
        return tuple(gathered[index] for index in range(count))

    members = block_list[0].reshape(-1)
    present = members >= 0
    source_dev = jnp.where(present, members // block_count, -1)
    before = (
        present[None, :]
        & (source_dev[None, :] == source_dev[:, None])
        & (members[None, :] < members[:, None])
    )
    slot_at = jnp.sum(before, axis=1)
    recv_row = jnp.where(present, source_dev * slot_cap + slot_at, 0)

    arrived = lax.all_to_all(
        pack((queries, keys, values, cotangent)), "seq", split_axis=0, concat_axis=0, tiled=True
    )
    block_sums = jnp.sum(arrived[:, 1].astype(jnp.float32), axis=1)
    key_sum = jnp.sum(
        jnp.where(present[:, None], block_sums[recv_row], 0.0).reshape(
            groups_here, cluster_cap, head_dim
        ),
        axis=1,
    )
    summed = jnp.sum(lax.all_gather(key_sum, "dp"), axis=0)
    summed, arrived = lax.optimization_barrier((summed, arrived))
    present_count = jnp.sum(present.reshape(groups_here, cluster_cap).astype(jnp.int32), axis=1)
    outgoing = routed_attention(
        recv_row.reshape(groups_here, cluster_cap).astype(jnp.int32),
        present_count,
        jnp.where(present, members, 0).reshape(groups_here, cluster_cap).astype(jnp.int32),
        arrived,
    )
    returned = lax.all_to_all(outgoing, "seq", split_axis=0, concat_axis=0, tiled=True)
    centroid_next = decay_rate * centroid_sums + (1.0 - decay_rate) * summed
    return unpack(returned) + (centroid_next,)


def solution(mesh):
    in_specs = (
        P("dp", "seq", None),
        P("dp", "seq", None),
        P("dp", "seq", None),
        P("dp", "seq", None),
        P("dp", None, "seq"),
        P("dp", "seq", None),
        P("seq", None),
    )
    out_specs = (
        P("dp", "seq", None),
        P("dp", "seq", None),
        P("dp", "seq", None),
        P("dp", "seq", None),
        P("seq", None),
    )
    return jax.shard_map(
        per_device, mesh=mesh, in_specs=in_specs, out_specs=out_specs, check_vma=False
    )
```

```python
import math

import jax
import jax.numpy as jnp
from jax import lax
from jax.experimental import pallas as pl
from jax.experimental.pallas import tpu as pltpu
from jax.sharding import PartitionSpec as P

decay_rate = 0.99
neg_fill = -1e30


def attend_block(q, k, v, g, query_pos, key_pos):
    score_scale = 1.0 / math.sqrt(q.shape[-1])
    scores = (
        lax.dot_general(q, k, (((1,), (1,)), ((), ())), preferred_element_type=jnp.float32)
        * score_scale
    )
    visible = key_pos <= query_pos
    scores = jnp.where(visible, scores, neg_fill)
    row_max = jnp.max(scores, axis=-1, keepdims=True)
    raised = jnp.exp(scores - row_max)
    probabilities = jnp.where(visible, raised / jnp.sum(raised, axis=-1, keepdims=True), 0.0)
    weights = probabilities.astype(jnp.bfloat16)
    out_full = jnp.dot(weights, v, preferred_element_type=jnp.float32)
    dprobs = lax.dot_general(g, v, (((1,), (1,)), ((), ())), preferred_element_type=jnp.float32)
    row_dot = jnp.sum(g.astype(jnp.float32) * out_full, axis=-1, keepdims=True)
    dscores_wide = probabilities * (dprobs - row_dot) * score_scale
    dscores = dscores_wide.astype(jnp.bfloat16)
    grad_values = jnp.dot(
        probabilities.T.astype(jnp.bfloat16), g, preferred_element_type=jnp.float32
    )
    grad_queries = jnp.dot(dscores, k, preferred_element_type=jnp.float32)
    grad_keys = jnp.dot(dscores_wide.T.astype(jnp.bfloat16), q, preferred_element_type=jnp.float32)
    return (out_full, grad_queries, grad_keys, grad_values)


def routed_kernel(recv_ref, count_ref, member_ref, arrived_ref, out_ref):
    cluster_count, cluster_cap = member_ref.shape
    block_len = arrived_ref.shape[2]
    out_ref[...] = jnp.zeros(out_ref.shape, out_ref.dtype)

    def one_cluster(cluster, carry):
        present_count = count_ref[cluster]
        for used in range(1, cluster_cap + 1):

            @pl.when(present_count == used)
            def _():
                rows = [recv_ref[cluster, slot] for slot in range(used)]
                tiles = [
                    jnp.concatenate([arrived_ref[row, index] for row in rows], axis=0)
                    for index in range(4)
                ]
                offsets = lax.broadcasted_iota(jnp.int32, (used * block_len, 1), 0)
                query_pos = offsets % block_len
                key_offsets = lax.broadcasted_iota(jnp.int32, (1, used * block_len), 1)
                key_pos = key_offsets % block_len
                for slot in range(used):
                    base = member_ref[cluster, slot] * block_len
                    query_pos = jnp.where(offsets // block_len == slot, query_pos + base, query_pos)
                    key_pos = jnp.where(key_offsets // block_len == slot, key_pos + base, key_pos)
                results = attend_block(*tiles, query_pos, key_pos)
                for slot in range(used):
                    for index in range(4):
                        out_ref[rows[slot], index] = results[index][
                            slot * block_len : (slot + 1) * block_len
                        ].astype(out_ref.dtype)

        return carry

    lax.fori_loop(0, cluster_count, one_cluster, 0)


def routed_attention(recv_table, present_count, member_table, arrived):
    smem = pl.BlockSpec(memory_space=pltpu.SMEM)
    vmem = pl.BlockSpec(memory_space=pltpu.VMEM)
    return pl.pallas_call(
        routed_kernel,
        out_shape=jax.ShapeDtypeStruct(arrived.shape, arrived.dtype),
        in_specs=[smem, smem, smem, vmem],
        out_specs=vmem,
    )(recv_table, present_count, member_table, arrived)


def per_device(queries, keys, values, cotangent, cluster_of, block_list, centroid_sums):
    seq_size = lax.axis_size("seq")
    head_count = cluster_of.shape[1]
    block_count = cluster_of.shape[2]
    token_count = queries.shape[1]
    block_len = token_count // block_count
    head_dim = centroid_sums.shape[1]
    groups_here = block_list.shape[1]
    cluster_cap = block_list.shape[2]
    owner_count = seq_size // head_count
    slot_cap = min(block_count, max(1, 2 * block_count // owner_count))
    cluster_ids = cluster_of[0]
    owner_local = cluster_ids // groups_here
    earlier = jnp.arange(block_count)[:, None] < jnp.arange(block_count)[None, :]
    same_owner = owner_local[:, :, None] == owner_local[:, None, :]
    slot_of = jnp.sum(same_owner & earlier[None], axis=1)
    selector = owner_local[:, None, None, :] == jnp.arange(owner_count)[None, :, None, None]
    selector = selector & (slot_of[:, None, None, :] == jnp.arange(slot_cap)[None, None, :, None])
    selector = selector.astype(jnp.bfloat16)

    def pack(sources):
        stacked = jnp.stack([item[0] for item in sources])
        blocks_in = stacked.reshape(len(sources), block_count, block_len, head_count, head_dim)
        outgoing = jnp.einsum(
            "hlcj,ajthd->hlcatd", selector, blocks_in, preferred_element_type=jnp.float32
        )
        return outgoing.astype(jnp.bfloat16).reshape(
            seq_size * slot_cap, len(sources), block_len, head_dim
        )

    def unpack(returned):
        arranged = returned.reshape(head_count, owner_count, slot_cap, -1, block_len, head_dim)
        gathered = (
            jnp.einsum(
                "hlcj,hlctd->jthd",
                selector,
                arranged[:, :, :, index],
                preferred_element_type=jnp.float32,
            )
            for index in range(arranged.shape[3])
        )
        return tuple(
            item.astype(jnp.bfloat16).reshape(1, token_count, head_count * head_dim)
            for item in gathered
        )

    members = block_list[0].reshape(-1)
    present = members >= 0
    source_dev = jnp.where(present, members // block_count, -1)
    before = (
        present[None, :]
        & (source_dev[None, :] == source_dev[:, None])
        & (members[None, :] < members[:, None])
    )
    slot_at = jnp.sum(before, axis=1)
    recv_row = jnp.where(present, source_dev * slot_cap + slot_at, 0)

    arrived = lax.all_to_all(
        pack((queries, keys, values, cotangent)), "seq", split_axis=0, concat_axis=0, tiled=True
    )
    block_sums = jnp.sum(arrived[:, 1].astype(jnp.float32), axis=1)
    key_sum = jnp.sum(
        jnp.where(present[:, None], block_sums[recv_row], 0.0).reshape(
            groups_here, cluster_cap, head_dim
        ),
        axis=1,
    )
    dp_size = lax.axis_size("dp")
    summed = key_sum
    stride = 1
    while stride < dp_size:
        summed = summed + lax.ppermute(
            summed, "dp", [(index, index ^ stride) for index in range(dp_size)]
        )
        stride *= 2
    present_count = jnp.sum(present.reshape(groups_here, cluster_cap).astype(jnp.int32), axis=1)
    outgoing = routed_attention(
        recv_row.reshape(groups_here, cluster_cap).astype(jnp.int32),
        present_count,
        jnp.where(present, members, 0).reshape(groups_here, cluster_cap).astype(jnp.int32),
        arrived,
    )
    outgoing, summed = lax.optimization_barrier((outgoing, summed))
    returned = lax.all_to_all(outgoing, "seq", split_axis=0, concat_axis=0, tiled=True)
    centroid_next = decay_rate * centroid_sums + (1.0 - decay_rate) * summed
    return unpack(returned) + (centroid_next,)


def solution(mesh):
    in_specs = (
        P("dp", "seq", None),
        P("dp", "seq", None),
        P("dp", "seq", None),
        P("dp", "seq", None),
        P("dp", None, "seq"),
        P("dp", "seq", None),
        P("seq", None),
    )
    out_specs = (
        P("dp", "seq", None),
        P("dp", "seq", None),
        P("dp", "seq", None),
        P("dp", "seq", None),
        P("seq", None),
    )
    return jax.shard_map(
        per_device, mesh=mesh, in_specs=in_specs, out_specs=out_specs, check_vma=False
    )
```

```python
import math

import jax
import jax.numpy as jnp
from jax import lax
from jax.experimental import pallas as pl
from jax.experimental.pallas import tpu as pltpu
from jax.sharding import PartitionSpec as P

decay_rate = 0.99
neg_fill = -1e30


def attend_block(q, k, v, g, query_pos, key_pos):
    score_scale = 1.0 / math.sqrt(q.shape[-1])
    scores = (
        lax.dot_general(q, k, (((1,), (1,)), ((), ())), preferred_element_type=jnp.float32)
        * score_scale
    )
    visible = key_pos <= query_pos
    scores = jnp.where(visible, scores, neg_fill)
    row_max = jnp.max(scores, axis=-1, keepdims=True)
    raised = jnp.exp(scores - row_max)
    probabilities = jnp.where(visible, raised / jnp.sum(raised, axis=-1, keepdims=True), 0.0)
    weights = probabilities.astype(jnp.bfloat16)
    out_full = jnp.dot(weights, v, preferred_element_type=jnp.float32)
    dprobs = lax.dot_general(g, v, (((1,), (1,)), ((), ())), preferred_element_type=jnp.float32)
    row_dot = jnp.sum(g.astype(jnp.float32) * out_full, axis=-1, keepdims=True)
    dscores_wide = probabilities * (dprobs - row_dot) * score_scale
    dscores = dscores_wide.astype(jnp.bfloat16)
    grad_values = jnp.dot(
        probabilities.T.astype(jnp.bfloat16), g, preferred_element_type=jnp.float32
    )
    grad_queries = jnp.dot(dscores, k, preferred_element_type=jnp.float32)
    grad_keys = jnp.dot(dscores_wide.T.astype(jnp.bfloat16), q, preferred_element_type=jnp.float32)
    return (out_full, grad_queries, grad_keys, grad_values)


def routed_kernel(recv_ref, count_ref, member_ref, arrived_ref, out_ref):
    cluster_count, cluster_cap = member_ref.shape
    block_len = arrived_ref.shape[2]
    out_ref[...] = jnp.zeros(out_ref.shape, out_ref.dtype)

    def one_cluster(cluster, carry):
        present_count = count_ref[cluster]
        for used in range(1, cluster_cap + 1):

            @pl.when(present_count == used)
            def _():
                rows = [recv_ref[cluster, slot] for slot in range(used)]
                tiles = [
                    jnp.concatenate([arrived_ref[row, index] for row in rows], axis=0)
                    for index in range(4)
                ]
                offsets = lax.broadcasted_iota(jnp.int32, (used * block_len, 1), 0)
                query_pos = offsets % block_len
                key_offsets = lax.broadcasted_iota(jnp.int32, (1, used * block_len), 1)
                key_pos = key_offsets % block_len
                for slot in range(used):
                    base = member_ref[cluster, slot] * block_len
                    query_pos = jnp.where(offsets // block_len == slot, query_pos + base, query_pos)
                    key_pos = jnp.where(key_offsets // block_len == slot, key_pos + base, key_pos)
                results = attend_block(*tiles, query_pos, key_pos)
                for slot in range(used):
                    for index in range(4):
                        out_ref[rows[slot], index] = results[index][
                            slot * block_len : (slot + 1) * block_len
                        ].astype(out_ref.dtype)

        return carry

    lax.fori_loop(0, cluster_count, one_cluster, 0)


def routed_attention(recv_table, present_count, member_table, arrived):
    smem = pl.BlockSpec(memory_space=pltpu.SMEM)
    vmem = pl.BlockSpec(memory_space=pltpu.VMEM)
    return pl.pallas_call(
        routed_kernel,
        out_shape=jax.ShapeDtypeStruct(arrived.shape, arrived.dtype),
        in_specs=[smem, smem, smem, vmem],
        out_specs=vmem,
    )(recv_table, present_count, member_table, arrived)


def pack_kernel(dest_ref, *refs):
    in_refs, out_ref = refs[:-1], refs[-1]
    head_count, block_count = dest_ref.shape
    block_len = out_ref.shape[2]
    head_dim = out_ref.shape[3]
    out_ref[...] = jnp.zeros(out_ref.shape, out_ref.dtype)
    for head in range(head_count):
        for block in range(block_count):
            slot = dest_ref[head, block]
            for index, in_ref in enumerate(in_refs):
                out_ref[slot, index] = in_ref[
                    block * block_len : (block + 1) * block_len,
                    head * head_dim : (head + 1) * head_dim,
                ]


def unpack_kernel(dest_ref, in_ref, *out_refs):
    head_count, block_count = dest_ref.shape
    block_len = in_ref.shape[2]
    head_dim = in_ref.shape[3]
    for head in range(head_count):
        for block in range(block_count):
            slot = dest_ref[head, block]
            for index, out_ref in enumerate(out_refs):
                out_ref[
                    block * block_len : (block + 1) * block_len,
                    head * head_dim : (head + 1) * head_dim,
                ] = in_ref[slot, index]


def pack_blocks(dest_table, sources, slot_count, block_len):
    smem = pl.BlockSpec(memory_space=pltpu.SMEM)
    vmem = pl.BlockSpec(memory_space=pltpu.VMEM)
    head_dim = sources[0].shape[1] // dest_table.shape[0]
    return pl.pallas_call(
        pack_kernel,
        out_shape=jax.ShapeDtypeStruct(
            (slot_count, len(sources), block_len, head_dim), sources[0].dtype
        ),
        in_specs=[smem] + [vmem] * len(sources),
        out_specs=vmem,
    )(dest_table, *sources)


def unpack_blocks(dest_table, returned, token_count):
    smem = pl.BlockSpec(memory_space=pltpu.SMEM)
    vmem = pl.BlockSpec(memory_space=pltpu.VMEM)
    width = dest_table.shape[0] * returned.shape[3]
    count = returned.shape[1]
    return pl.pallas_call(
        unpack_kernel,
        out_shape=tuple(
            jax.ShapeDtypeStruct((token_count, width), returned.dtype) for _ in range(count)
        ),
        in_specs=[smem, vmem],
        out_specs=tuple(vmem for _ in range(count)),
    )(dest_table, returned)


def per_device(queries, keys, values, cotangent, cluster_of, block_list, centroid_sums):
    seq_size = lax.axis_size("seq")
    head_count = cluster_of.shape[1]
    block_count = cluster_of.shape[2]
    token_count = queries.shape[1]
    block_len = token_count // block_count
    head_dim = centroid_sums.shape[1]
    groups_here = block_list.shape[1]
    cluster_cap = block_list.shape[2]
    owner_count = seq_size // head_count
    slot_cap = min(block_count, max(1, 2 * block_count // owner_count))
    cluster_ids = cluster_of[0]
    owner_local = cluster_ids // groups_here
    earlier = jnp.arange(block_count)[:, None] < jnp.arange(block_count)[None, :]
    same_owner = owner_local[:, :, None] == owner_local[:, None, :]
    slot_of = jnp.sum(same_owner & earlier[None], axis=1)
    dest_table = (
        owner_local * slot_cap + jnp.minimum(slot_of, slot_cap - 1)
    ).astype(jnp.int32) + (jnp.arange(head_count) * owner_count * slot_cap)[:, None].astype(jnp.int32)

    members = block_list[0].reshape(-1)
    present = members >= 0
    source_dev = jnp.where(present, members // block_count, -1)
    before = (
        present[None, :]
        & (source_dev[None, :] == source_dev[:, None])
        & (members[None, :] < members[:, None])
    )
    slot_at = jnp.sum(before, axis=1)
    recv_row = jnp.where(present, source_dev * slot_cap + slot_at, 0)

    arrived = lax.all_to_all(
        pack_blocks(
            dest_table,
            (queries[0], keys[0], values[0], cotangent[0]),
            seq_size * slot_cap,
            block_len,
        ),
        "seq",
        split_axis=0,
        concat_axis=0,
        tiled=True,
    )
    block_sums = jnp.sum(arrived[:, 1].astype(jnp.float32), axis=1)
    key_sum = jnp.sum(
        jnp.where(present[:, None], block_sums[recv_row], 0.0).reshape(
            groups_here, cluster_cap, head_dim
        ),
        axis=1,
    )
    dp_size = lax.axis_size("dp")
    summed = key_sum
    stride = 1
    while stride < dp_size:
        summed = summed + lax.ppermute(
            summed, "dp", [(index, index ^ stride) for index in range(dp_size)]
        )
        stride *= 2
    present_count = jnp.sum(present.reshape(groups_here, cluster_cap).astype(jnp.int32), axis=1)
    outgoing = routed_attention(
        recv_row.reshape(groups_here, cluster_cap).astype(jnp.int32),
        present_count,
        jnp.where(present, members, 0).reshape(groups_here, cluster_cap).astype(jnp.int32),
        arrived,
    )
    outgoing, summed = lax.optimization_barrier((outgoing, summed))
    returned = lax.all_to_all(outgoing, "seq", split_axis=0, concat_axis=0, tiled=True)
    centroid_next = decay_rate * centroid_sums + (1.0 - decay_rate) * summed
    finished = unpack_blocks(dest_table, returned, token_count)
    return tuple(item[None] for item in finished) + (centroid_next,)


def solution(mesh):
    in_specs = (
        P("dp", "seq", None),
        P("dp", "seq", None),
        P("dp", "seq", None),
        P("dp", "seq", None),
        P("dp", None, "seq"),
        P("dp", "seq", None),
        P("seq", None),
    )
    out_specs = (
        P("dp", "seq", None),
        P("dp", "seq", None),
        P("dp", "seq", None),
        P("dp", "seq", None),
        P("seq", None),
    )
    return jax.shard_map(
        per_device, mesh=mesh, in_specs=in_specs, out_specs=out_specs, check_vma=False
    )
```

```python
import math

import jax
import jax.numpy as jnp
from jax import lax
from jax.experimental import pallas as pl
from jax.experimental.pallas import tpu as pltpu
from jax.sharding import PartitionSpec as P

decay_rate = 0.99
neg_fill = -1e30


def attend_block(q, k, v, g, query_pos, key_pos):
    score_scale = 1.0 / math.sqrt(q.shape[-1])
    scores = (
        lax.dot_general(q, k, (((1,), (1,)), ((), ())), preferred_element_type=jnp.float32)
        * score_scale
    )
    visible = key_pos <= query_pos
    scores = jnp.where(visible, scores, neg_fill)
    row_max = jnp.max(scores, axis=-1, keepdims=True)
    raised = jnp.exp(scores - row_max)
    probabilities = jnp.where(visible, raised / jnp.sum(raised, axis=-1, keepdims=True), 0.0)
    weights = probabilities.astype(jnp.bfloat16)
    out_full = jnp.dot(weights, v, preferred_element_type=jnp.float32)
    dprobs = lax.dot_general(g, v, (((1,), (1,)), ((), ())), preferred_element_type=jnp.float32)
    row_dot = jnp.sum(g.astype(jnp.float32) * out_full, axis=-1, keepdims=True)
    dscores_wide = probabilities * (dprobs - row_dot) * score_scale
    dscores = dscores_wide.astype(jnp.bfloat16)
    grad_values = jnp.dot(
        probabilities.T.astype(jnp.bfloat16), g, preferred_element_type=jnp.float32
    )
    grad_queries = jnp.dot(dscores, k, preferred_element_type=jnp.float32)
    grad_keys = jnp.dot(dscores_wide.T.astype(jnp.bfloat16), q, preferred_element_type=jnp.float32)
    return (out_full, grad_queries, grad_keys, grad_values)


def routed_kernel(recv_ref, count_ref, member_ref, arrived_ref, out_ref):
    cluster_count, cluster_cap = member_ref.shape
    block_len = arrived_ref.shape[2]
    out_ref[...] = jnp.zeros(out_ref.shape, out_ref.dtype)

    def one_cluster(cluster, carry):
        present_count = count_ref[cluster]
        for used in range(1, cluster_cap + 1):

            @pl.when(present_count == used)
            def _():
                rows = [recv_ref[cluster, slot] for slot in range(used)]
                tiles = [
                    jnp.concatenate([arrived_ref[row, index] for row in rows], axis=0)
                    for index in range(4)
                ]
                offsets = lax.broadcasted_iota(jnp.int32, (used * block_len, 1), 0)
                query_pos = offsets % block_len
                key_offsets = lax.broadcasted_iota(jnp.int32, (1, used * block_len), 1)
                key_pos = key_offsets % block_len
                for slot in range(used):
                    base = member_ref[cluster, slot] * block_len
                    query_pos = jnp.where(offsets // block_len == slot, query_pos + base, query_pos)
                    key_pos = jnp.where(key_offsets // block_len == slot, key_pos + base, key_pos)
                results = attend_block(*tiles, query_pos, key_pos)
                for slot in range(used):
                    for index in range(4):
                        out_ref[rows[slot], index] = results[index][
                            slot * block_len : (slot + 1) * block_len
                        ].astype(out_ref.dtype)

        return carry

    lax.fori_loop(0, cluster_count, one_cluster, 0)


def routed_attention(recv_table, present_count, member_table, arrived):
    smem = pl.BlockSpec(memory_space=pltpu.SMEM)
    vmem = pl.BlockSpec(memory_space=pltpu.VMEM)
    return pl.pallas_call(
        routed_kernel,
        out_shape=jax.ShapeDtypeStruct(arrived.shape, arrived.dtype),
        in_specs=[smem, smem, smem, vmem],
        out_specs=vmem,
    )(recv_table, present_count, member_table, arrived)


def pack_kernel(dest_ref, *refs):
    in_refs, out_ref = refs[:-1], refs[-1]
    head_count, block_count = dest_ref.shape
    block_len = out_ref.shape[2]
    head_dim = out_ref.shape[3]
    out_ref[...] = jnp.zeros(out_ref.shape, out_ref.dtype)
    for head in range(head_count):
        for block in range(block_count):
            slot = dest_ref[head, block]
            for index, in_ref in enumerate(in_refs):
                out_ref[slot, index] = in_ref[
                    block * block_len : (block + 1) * block_len,
                    head * head_dim : (head + 1) * head_dim,
                ]


def unpack_kernel(dest_ref, in_ref, *out_refs):
    head_count, block_count = dest_ref.shape
    block_len = in_ref.shape[2]
    head_dim = in_ref.shape[3]
    for head in range(head_count):
        for block in range(block_count):
            slot = dest_ref[head, block]
            for index, out_ref in enumerate(out_refs):
                out_ref[
                    block * block_len : (block + 1) * block_len,
                    head * head_dim : (head + 1) * head_dim,
                ] = in_ref[slot, index]


def pack_blocks(dest_table, sources, slot_count, block_len):
    smem = pl.BlockSpec(memory_space=pltpu.SMEM)
    vmem = pl.BlockSpec(memory_space=pltpu.VMEM)
    head_dim = sources[0].shape[1] // dest_table.shape[0]
    return pl.pallas_call(
        pack_kernel,
        out_shape=jax.ShapeDtypeStruct(
            (slot_count, len(sources), block_len, head_dim), sources[0].dtype
        ),
        in_specs=[smem] + [vmem] * len(sources),
        out_specs=vmem,
    )(dest_table, *sources)


def unpack_blocks(dest_table, returned, token_count):
    smem = pl.BlockSpec(memory_space=pltpu.SMEM)
    vmem = pl.BlockSpec(memory_space=pltpu.VMEM)
    width = dest_table.shape[0] * returned.shape[3]
    count = returned.shape[1]
    return pl.pallas_call(
        unpack_kernel,
        out_shape=tuple(
            jax.ShapeDtypeStruct((token_count, width), returned.dtype) for _ in range(count)
        ),
        in_specs=[smem, vmem],
        out_specs=tuple(vmem for _ in range(count)),
    )(dest_table, returned)


def per_device(queries, keys, values, cotangent, cluster_of, block_list, centroid_sums):
    seq_size = lax.axis_size("seq")
    head_count = cluster_of.shape[1]
    block_count = cluster_of.shape[2]
    token_count = queries.shape[1]
    block_len = token_count // block_count
    head_dim = centroid_sums.shape[1]
    groups_here = block_list.shape[1]
    cluster_cap = block_list.shape[2]
    owner_count = seq_size // head_count
    slot_cap = min(block_count, max(1, 2 * block_count // owner_count))
    cluster_ids = cluster_of[0]
    owner_local = cluster_ids // groups_here
    earlier = jnp.arange(block_count)[:, None] < jnp.arange(block_count)[None, :]
    same_owner = owner_local[:, :, None] == owner_local[:, None, :]
    slot_of = jnp.sum(same_owner & earlier[None], axis=1)
    dest_table = (
        owner_local * slot_cap + jnp.minimum(slot_of, slot_cap - 1)
    ).astype(jnp.int32) + (jnp.arange(head_count) * owner_count * slot_cap)[:, None].astype(jnp.int32)

    members = block_list[0].reshape(-1)
    present = members >= 0
    source_dev = jnp.where(present, members // block_count, -1)
    before = (
        present[None, :]
        & (source_dev[None, :] == source_dev[:, None])
        & (members[None, :] < members[:, None])
    )
    slot_at = jnp.sum(before, axis=1)
    recv_row = jnp.where(present, source_dev * slot_cap + slot_at, 0)

    arrived = lax.all_to_all(
        pack_blocks(
            dest_table,
            (queries[0], keys[0], values[0], cotangent[0]),
            seq_size * slot_cap,
            block_len,
        ),
        "seq",
        split_axis=0,
        concat_axis=0,
        tiled=True,
    )
    block_sums = jnp.sum(arrived[:, 1].astype(jnp.float32), axis=1)
    key_sum = jnp.sum(
        jnp.where(present[:, None], block_sums[recv_row], 0.0).reshape(
            groups_here, cluster_cap, head_dim
        ),
        axis=1,
    )
    present_count = jnp.sum(present.reshape(groups_here, cluster_cap).astype(jnp.int32), axis=1)
    outgoing = routed_attention(
        recv_row.reshape(groups_here, cluster_cap).astype(jnp.int32),
        present_count,
        jnp.where(present, members, 0).reshape(groups_here, cluster_cap).astype(jnp.int32),
        arrived,
    )
    outgoing, key_sum = lax.optimization_barrier((outgoing, key_sum))
    dp_size = lax.axis_size("dp")
    summed = key_sum
    stride = 1
    while stride < dp_size:
        summed = summed + lax.ppermute(
            summed, "dp", [(index, index ^ stride) for index in range(dp_size)]
        )
        stride *= 2
    returned = lax.all_to_all(outgoing, "seq", split_axis=0, concat_axis=0, tiled=True)
    centroid_next = decay_rate * centroid_sums + (1.0 - decay_rate) * summed
    finished = unpack_blocks(dest_table, returned, token_count)
    return tuple(item[None] for item in finished) + (centroid_next,)


def solution(mesh):
    in_specs = (
        P("dp", "seq", None),
        P("dp", "seq", None),
        P("dp", "seq", None),
        P("dp", "seq", None),
        P("dp", None, "seq"),
        P("dp", "seq", None),
        P("seq", None),
    )
    out_specs = (
        P("dp", "seq", None),
        P("dp", "seq", None),
        P("dp", "seq", None),
        P("dp", "seq", None),
        P("seq", None),
    )
    return jax.shard_map(
        per_device, mesh=mesh, in_specs=in_specs, out_specs=out_specs, check_vma=False
    )
```

```python
import math

import jax
import jax.numpy as jnp
from jax import lax
from jax.experimental import pallas as pl
from jax.experimental.pallas import tpu as pltpu
from jax.sharding import PartitionSpec as P

decay_rate = 0.99
neg_fill = -1e30


def attend_block(q, k, v, g, query_pos, key_pos):
    score_scale = 1.0 / math.sqrt(q.shape[-1])
    scores = (
        lax.dot_general(q, k, (((1,), (1,)), ((), ())), preferred_element_type=jnp.float32)
        * score_scale
    )
    visible = key_pos <= query_pos
    scores = jnp.where(visible, scores, neg_fill)
    row_max = jnp.max(scores, axis=-1, keepdims=True)
    raised = jnp.exp(scores - row_max)
    probabilities = jnp.where(visible, raised / jnp.sum(raised, axis=-1, keepdims=True), 0.0)
    weights = probabilities.astype(jnp.bfloat16)
    out_full = jnp.dot(weights, v, preferred_element_type=jnp.float32)
    dprobs = lax.dot_general(g, v, (((1,), (1,)), ((), ())), preferred_element_type=jnp.float32)
    row_dot = jnp.sum(g.astype(jnp.float32) * out_full, axis=-1, keepdims=True)
    dscores_wide = probabilities * (dprobs - row_dot) * score_scale
    dscores = dscores_wide.astype(jnp.bfloat16)
    grad_values = jnp.dot(
        probabilities.T.astype(jnp.bfloat16), g, preferred_element_type=jnp.float32
    )
    grad_queries = jnp.dot(dscores, k, preferred_element_type=jnp.float32)
    grad_keys = jnp.dot(dscores_wide.T.astype(jnp.bfloat16), q, preferred_element_type=jnp.float32)
    return (out_full, grad_queries, grad_keys, grad_values)


def routed_kernel(recv_ref, count_ref, member_ref, arrived_ref, out_ref):
    cluster_count, cluster_cap = member_ref.shape
    block_len = arrived_ref.shape[2]
    out_ref[...] = jnp.zeros(out_ref.shape, out_ref.dtype)

    def one_cluster(cluster, carry):
        present_count = count_ref[cluster]
        for used in range(1, cluster_cap + 1):

            @pl.when(present_count == used)
            def _():
                rows = [recv_ref[cluster, slot] for slot in range(used)]
                tiles = [
                    jnp.concatenate([arrived_ref[row, index] for row in rows], axis=0)
                    for index in range(4)
                ]
                offsets = lax.broadcasted_iota(jnp.int32, (used * block_len, 1), 0)
                query_pos = offsets % block_len
                key_offsets = lax.broadcasted_iota(jnp.int32, (1, used * block_len), 1)
                key_pos = key_offsets % block_len
                for slot in range(used):
                    base = member_ref[cluster, slot] * block_len
                    query_pos = jnp.where(offsets // block_len == slot, query_pos + base, query_pos)
                    key_pos = jnp.where(key_offsets // block_len == slot, key_pos + base, key_pos)
                results = attend_block(*tiles, query_pos, key_pos)
                for slot in range(used):
                    for index in range(4):
                        out_ref[rows[slot], index] = results[index][
                            slot * block_len : (slot + 1) * block_len
                        ].astype(out_ref.dtype)

        return carry

    lax.fori_loop(0, cluster_count, one_cluster, 0)


def routed_attention(recv_table, present_count, member_table, arrived):
    smem = pl.BlockSpec(memory_space=pltpu.SMEM)
    vmem = pl.BlockSpec(memory_space=pltpu.VMEM)
    return pl.pallas_call(
        routed_kernel,
        out_shape=jax.ShapeDtypeStruct(arrived.shape, arrived.dtype),
        in_specs=[smem, smem, smem, vmem],
        out_specs=vmem,
    )(recv_table, present_count, member_table, arrived)


def pack_kernel(dest_ref, *refs):
    in_refs, out_ref = refs[:-1], refs[-1]
    head_count, block_count = dest_ref.shape
    block_len = out_ref.shape[2]
    head_dim = out_ref.shape[3]
    out_ref[...] = jnp.zeros(out_ref.shape, out_ref.dtype)
    for head in range(head_count):
        for block in range(block_count):
            slot = dest_ref[head, block]
            for index, in_ref in enumerate(in_refs):
                out_ref[slot, index] = in_ref[
                    block * block_len : (block + 1) * block_len,
                    head * head_dim : (head + 1) * head_dim,
                ]


def unpack_kernel(dest_ref, in_ref, *out_refs):
    head_count, block_count = dest_ref.shape
    block_len = in_ref.shape[2]
    head_dim = in_ref.shape[3]
    for head in range(head_count):
        for block in range(block_count):
            slot = dest_ref[head, block]
            for index, out_ref in enumerate(out_refs):
                out_ref[
                    block * block_len : (block + 1) * block_len,
                    head * head_dim : (head + 1) * head_dim,
                ] = in_ref[slot, index]


def pack_blocks(dest_table, sources, slot_count, block_len):
    smem = pl.BlockSpec(memory_space=pltpu.SMEM)
    vmem = pl.BlockSpec(memory_space=pltpu.VMEM)
    head_dim = sources[0].shape[1] // dest_table.shape[0]
    return pl.pallas_call(
        pack_kernel,
        out_shape=jax.ShapeDtypeStruct(
            (slot_count, len(sources), block_len, head_dim), sources[0].dtype
        ),
        in_specs=[smem] + [vmem] * len(sources),
        out_specs=vmem,
    )(dest_table, *sources)


def unpack_blocks(dest_table, returned, token_count):
    smem = pl.BlockSpec(memory_space=pltpu.SMEM)
    vmem = pl.BlockSpec(memory_space=pltpu.VMEM)
    width = dest_table.shape[0] * returned.shape[3]
    count = returned.shape[1]
    return pl.pallas_call(
        unpack_kernel,
        out_shape=tuple(
            jax.ShapeDtypeStruct((token_count, width), returned.dtype) for _ in range(count)
        ),
        in_specs=[smem, vmem],
        out_specs=tuple(vmem for _ in range(count)),
    )(dest_table, returned)


def per_device(queries, keys, values, cotangent, cluster_of, block_list, centroid_sums):
    seq_size = lax.axis_size("seq")
    head_count = cluster_of.shape[1]
    block_count = cluster_of.shape[2]
    token_count = queries.shape[1]
    block_len = token_count // block_count
    head_dim = centroid_sums.shape[1]
    groups_here = block_list.shape[1]
    cluster_cap = block_list.shape[2]
    owner_count = seq_size // head_count
    slot_cap = min(block_count, max(1, 2 * block_count // owner_count))
    cluster_ids = cluster_of[0]
    owner_local = cluster_ids // groups_here
    earlier = jnp.arange(block_count)[:, None] < jnp.arange(block_count)[None, :]
    same_owner = owner_local[:, :, None] == owner_local[:, None, :]
    slot_of = jnp.sum(same_owner & earlier[None], axis=1)
    dest_table = (
        owner_local * slot_cap + jnp.minimum(slot_of, slot_cap - 1)
    ).astype(jnp.int32) + (jnp.arange(head_count) * owner_count * slot_cap)[:, None].astype(jnp.int32)

    members = block_list[0].reshape(-1)
    present = members >= 0
    source_dev = jnp.where(present, members // block_count, -1)
    before = (
        present[None, :]
        & (source_dev[None, :] == source_dev[:, None])
        & (members[None, :] < members[:, None])
    )
    slot_at = jnp.sum(before, axis=1)
    recv_row = jnp.where(present, source_dev * slot_cap + slot_at, 0)

    arrived = lax.all_to_all(
        pack_blocks(
            dest_table,
            (queries[0], keys[0], values[0], cotangent[0]),
            seq_size * slot_cap,
            block_len,
        ),
        "seq",
        split_axis=0,
        concat_axis=0,
        tiled=True,
    )
    block_sums = jnp.sum(arrived[:, 1].astype(jnp.float32), axis=1)
    key_sum = jnp.sum(
        jnp.where(present[:, None], block_sums[recv_row], 0.0).reshape(
            groups_here, cluster_cap, head_dim
        ),
        axis=1,
    )
    present_count = jnp.sum(present.reshape(groups_here, cluster_cap).astype(jnp.int32), axis=1)
    outgoing = routed_attention(
        recv_row.reshape(groups_here, cluster_cap).astype(jnp.int32),
        present_count,
        jnp.where(present, members, 0).reshape(groups_here, cluster_cap).astype(jnp.int32),
        arrived,
    )
    outgoing, key_sum = lax.optimization_barrier((outgoing, key_sum))
    dp_size = lax.axis_size("dp")
    received = jnp.stack(
        [key_sum]
        + [
            lax.ppermute(
                key_sum, "dp", [(index, (index + shift) % dp_size) for index in range(dp_size)]
            )
            for shift in range(1, dp_size)
        ]
    )
    dp_index = lax.axis_index("dp")
    summed = received[dp_index % dp_size]
    for source in range(1, dp_size):
        summed = summed + received[(dp_index - source) % dp_size]
    returned = lax.all_to_all(outgoing, "seq", split_axis=0, concat_axis=0, tiled=True)
    centroid_next = decay_rate * centroid_sums + (1.0 - decay_rate) * summed
    finished = unpack_blocks(dest_table, returned, token_count)
    return tuple(item[None] for item in finished) + (centroid_next,)


def solution(mesh):
    in_specs = (
        P("dp", "seq", None),
        P("dp", "seq", None),
        P("dp", "seq", None),
        P("dp", "seq", None),
        P("dp", None, "seq"),
        P("dp", "seq", None),
        P("seq", None),
    )
    out_specs = (
        P("dp", "seq", None),
        P("dp", "seq", None),
        P("dp", "seq", None),
        P("dp", "seq", None),
        P("seq", None),
    )
    return jax.shard_map(
        per_device, mesh=mesh, in_specs=in_specs, out_specs=out_specs, check_vma=False
    )
```

```python
import math

import jax
import jax.numpy as jnp
from jax import lax
from jax.experimental import pallas as pl
from jax.experimental.pallas import tpu as pltpu
from jax.sharding import PartitionSpec as P

decay_rate = 0.99
neg_fill = -1e30


def attend_block(q, k, v, g, query_pos, key_pos):
    score_scale = 1.0 / math.sqrt(q.shape[-1])
    scores = (
        lax.dot_general(q, k, (((1,), (1,)), ((), ())), preferred_element_type=jnp.float32)
        * score_scale
    )
    visible = key_pos <= query_pos
    scores = jnp.where(visible, scores, neg_fill)
    row_max = jnp.max(scores, axis=-1, keepdims=True)
    raised = jnp.exp(scores - row_max)
    probabilities = jnp.where(visible, raised / jnp.sum(raised, axis=-1, keepdims=True), 0.0)
    weights = probabilities.astype(jnp.bfloat16)
    out_full = jnp.dot(weights, v, preferred_element_type=jnp.float32)
    dprobs = lax.dot_general(g, v, (((1,), (1,)), ((), ())), preferred_element_type=jnp.float32)
    row_dot = jnp.sum(g.astype(jnp.float32) * out_full, axis=-1, keepdims=True)
    dscores = (probabilities * (dprobs - row_dot) * score_scale).astype(jnp.bfloat16)
    grad_values = lax.dot_general(
        weights, g, (((0,), (0,)), ((), ())), preferred_element_type=jnp.float32
    )
    grad_queries = jnp.dot(dscores, k, preferred_element_type=jnp.float32)
    grad_keys = lax.dot_general(
        dscores, q, (((0,), (0,)), ((), ())), preferred_element_type=jnp.float32
    )
    return (out_full, grad_queries, grad_keys, grad_values)


def routed_kernel(recv_ref, count_ref, member_ref, arrived_ref, out_ref):
    cluster_count, cluster_cap = member_ref.shape
    block_len = arrived_ref.shape[2]
    out_ref[...] = jnp.zeros(out_ref.shape, out_ref.dtype)

    def one_cluster(cluster, carry):
        present_count = count_ref[cluster]
        for used in range(1, cluster_cap + 1):

            @pl.when(present_count == used)
            def _():
                rows = [recv_ref[cluster, slot] for slot in range(used)]
                tiles = [
                    jnp.concatenate([arrived_ref[row, index] for row in rows], axis=0)
                    for index in range(4)
                ]
                offsets = lax.broadcasted_iota(jnp.int32, (used * block_len, 1), 0)
                query_pos = offsets % block_len
                key_offsets = lax.broadcasted_iota(jnp.int32, (1, used * block_len), 1)
                key_pos = key_offsets % block_len
                for slot in range(used):
                    base = member_ref[cluster, slot] * block_len
                    query_pos = jnp.where(offsets // block_len == slot, query_pos + base, query_pos)
                    key_pos = jnp.where(key_offsets // block_len == slot, key_pos + base, key_pos)
                results = attend_block(*tiles, query_pos, key_pos)
                for slot in range(used):
                    for index in range(4):
                        out_ref[rows[slot], index] = results[index][
                            slot * block_len : (slot + 1) * block_len
                        ].astype(out_ref.dtype)

        return carry

    lax.fori_loop(0, cluster_count, one_cluster, 0)


def routed_attention(recv_table, present_count, member_table, arrived):
    smem = pl.BlockSpec(memory_space=pltpu.SMEM)
    vmem = pl.BlockSpec(memory_space=pltpu.VMEM)
    return pl.pallas_call(
        routed_kernel,
        out_shape=jax.ShapeDtypeStruct(arrived.shape, arrived.dtype),
        in_specs=[smem, smem, smem, vmem],
        out_specs=vmem,
    )(recv_table, present_count, member_table, arrived)


def pack_kernel(dest_ref, *refs):
    in_refs, out_ref = refs[:-1], refs[-1]
    head_count, block_count = dest_ref.shape
    block_len = out_ref.shape[2]
    head_dim = out_ref.shape[3]
    out_ref[...] = jnp.zeros(out_ref.shape, out_ref.dtype)
    for head in range(head_count):
        for block in range(block_count):
            slot = dest_ref[head, block]
            for index, in_ref in enumerate(in_refs):
                out_ref[slot, index] = in_ref[
                    block * block_len : (block + 1) * block_len,
                    head * head_dim : (head + 1) * head_dim,
                ]


def unpack_kernel(dest_ref, in_ref, *out_refs):
    head_count, block_count = dest_ref.shape
    block_len = in_ref.shape[2]
    head_dim = in_ref.shape[3]
    for head in range(head_count):
        for block in range(block_count):
            slot = dest_ref[head, block]
            for index, out_ref in enumerate(out_refs):
                out_ref[
                    block * block_len : (block + 1) * block_len,
                    head * head_dim : (head + 1) * head_dim,
                ] = in_ref[slot, index]


def pack_blocks(dest_table, sources, slot_count, block_len):
    smem = pl.BlockSpec(memory_space=pltpu.SMEM)
    vmem = pl.BlockSpec(memory_space=pltpu.VMEM)
    head_dim = sources[0].shape[1] // dest_table.shape[0]
    return pl.pallas_call(
        pack_kernel,
        out_shape=jax.ShapeDtypeStruct(
            (slot_count, len(sources), block_len, head_dim), sources[0].dtype
        ),
        in_specs=[smem] + [vmem] * len(sources),
        out_specs=vmem,
    )(dest_table, *sources)


def unpack_blocks(dest_table, returned, token_count):
    smem = pl.BlockSpec(memory_space=pltpu.SMEM)
    vmem = pl.BlockSpec(memory_space=pltpu.VMEM)
    width = dest_table.shape[0] * returned.shape[3]
    count = returned.shape[1]
    return pl.pallas_call(
        unpack_kernel,
        out_shape=tuple(
            jax.ShapeDtypeStruct((token_count, width), returned.dtype) for _ in range(count)
        ),
        in_specs=[smem, vmem],
        out_specs=tuple(vmem for _ in range(count)),
    )(dest_table, returned)


def per_device(queries, keys, values, cotangent, cluster_of, block_list, centroid_sums):
    seq_size = lax.axis_size("seq")
    head_count = cluster_of.shape[1]
    block_count = cluster_of.shape[2]
    token_count = queries.shape[1]
    block_len = token_count // block_count
    head_dim = centroid_sums.shape[1]
    groups_here = block_list.shape[1]
    cluster_cap = block_list.shape[2]
    owner_count = seq_size // head_count
    slot_cap = min(block_count, max(1, 2 * block_count // owner_count))
    cluster_ids = cluster_of[0]
    owner_local = cluster_ids // groups_here
    earlier = jnp.arange(block_count)[:, None] < jnp.arange(block_count)[None, :]
    same_owner = owner_local[:, :, None] == owner_local[:, None, :]
    slot_of = jnp.sum(same_owner & earlier[None], axis=1)
    dest_table = (
        owner_local * slot_cap + jnp.minimum(slot_of, slot_cap - 1)
    ).astype(jnp.int32) + (jnp.arange(head_count) * owner_count * slot_cap)[:, None].astype(jnp.int32)

    members = block_list[0].reshape(-1)
    present = members >= 0
    source_dev = jnp.where(present, members // block_count, -1)
    before = (
        present[None, :]
        & (source_dev[None, :] == source_dev[:, None])
        & (members[None, :] < members[:, None])
    )
    slot_at = jnp.sum(before, axis=1)
    recv_row = jnp.where(present, source_dev * slot_cap + slot_at, 0)

    arrived = lax.all_to_all(
        pack_blocks(
            dest_table,
            (queries[0], keys[0], values[0], cotangent[0]),
            seq_size * slot_cap,
            block_len,
        ),
        "seq",
        split_axis=0,
        concat_axis=0,
        tiled=True,
    )
    block_sums = jnp.sum(arrived[:, 1].astype(jnp.float32), axis=1)
    key_sum = jnp.sum(
        jnp.where(present[:, None], block_sums[recv_row], 0.0).reshape(
            groups_here, cluster_cap, head_dim
        ),
        axis=1,
    )
    present_count = jnp.sum(present.reshape(groups_here, cluster_cap).astype(jnp.int32), axis=1)
    outgoing = routed_attention(
        recv_row.reshape(groups_here, cluster_cap).astype(jnp.int32),
        present_count,
        jnp.where(present, members, 0).reshape(groups_here, cluster_cap).astype(jnp.int32),
        arrived,
    )
    outgoing, key_sum = lax.optimization_barrier((outgoing, key_sum))
    dp_size = lax.axis_size("dp")
    received = jnp.stack(
        [key_sum]
        + [
            lax.ppermute(
                key_sum, "dp", [(index, (index + shift) % dp_size) for index in range(dp_size)]
            )
            for shift in range(1, dp_size)
        ]
    )
    dp_index = lax.axis_index("dp")
    summed = received[dp_index % dp_size]
    for source in range(1, dp_size):
        summed = summed + received[(dp_index - source) % dp_size]
    returned = lax.all_to_all(outgoing, "seq", split_axis=0, concat_axis=0, tiled=True)
    centroid_next = decay_rate * centroid_sums + (1.0 - decay_rate) * summed
    finished = unpack_blocks(dest_table, returned, token_count)
    return tuple(item[None] for item in finished) + (centroid_next,)


def solution(mesh):
    in_specs = (
        P("dp", "seq", None),
        P("dp", "seq", None),
        P("dp", "seq", None),
        P("dp", "seq", None),
        P("dp", None, "seq"),
        P("dp", "seq", None),
        P("seq", None),
    )
    out_specs = (
        P("dp", "seq", None),
        P("dp", "seq", None),
        P("dp", "seq", None),
        P("dp", "seq", None),
        P("seq", None),
    )
    return jax.shard_map(
        per_device, mesh=mesh, in_specs=in_specs, out_specs=out_specs, check_vma=False
    )
```

```python
import math

import jax
import jax.numpy as jnp
from jax import lax
from jax.experimental import pallas as pl
from jax.experimental.pallas import tpu as pltpu
from jax.sharding import PartitionSpec as P

decay_rate = 0.99
neg_fill = -1e30


def attend_block(q, k, v, g, query_pos, key_pos):
    score_scale = 1.0 / math.sqrt(q.shape[-1])
    scores = (
        lax.dot_general(q, k, (((1,), (1,)), ((), ())), preferred_element_type=jnp.float32)
        * score_scale
    )
    visible = key_pos <= query_pos
    scores = jnp.where(visible, scores, neg_fill)
    row_max = jnp.max(scores, axis=-1, keepdims=True)
    raised = jnp.exp(scores - row_max)
    probabilities = jnp.where(visible, raised / jnp.sum(raised, axis=-1, keepdims=True), 0.0)
    weights = probabilities.astype(jnp.bfloat16)
    out_full = jnp.dot(weights, v, preferred_element_type=jnp.float32)
    dprobs = lax.dot_general(g, v, (((1,), (1,)), ((), ())), preferred_element_type=jnp.float32)
    row_dot = jnp.sum(g.astype(jnp.float32) * out_full, axis=-1, keepdims=True)
    dscores = (probabilities * (dprobs - row_dot) * score_scale).astype(jnp.bfloat16)
    grad_values = lax.dot_general(
        weights, g, (((0,), (0,)), ((), ())), preferred_element_type=jnp.float32
    )
    grad_queries = jnp.dot(dscores, k, preferred_element_type=jnp.float32)
    grad_keys = lax.dot_general(
        dscores, q, (((0,), (0,)), ((), ())), preferred_element_type=jnp.float32
    )
    return (out_full, grad_queries, grad_keys, grad_values)


def routed_kernel(recv_ref, count_ref, member_ref, arrived_ref, out_ref):
    cluster_count, cluster_cap = member_ref.shape
    block_len = arrived_ref.shape[2]
    lanes = math.gcd(cluster_count, 2)
    stride = cluster_count // lanes
    out_ref[...] = jnp.zeros(out_ref.shape, out_ref.dtype)

    def one_step(step, carry):
        clusters = [step + lane * stride for lane in range(lanes)]
        counts = [count_ref[cluster] for cluster in clusters]
        widest = counts[0]
        for count in counts[1:]:
            widest = jnp.maximum(widest, count)
        for used in range(1, cluster_cap + 1):

            @pl.when(widest == used)
            def _():
                computed = []
                for cluster, count in zip(clusters, counts):
                    rows = [recv_ref[cluster, slot] for slot in range(used)]
                    tiles = [
                        jnp.concatenate([arrived_ref[row, index] for row in rows], axis=0)
                        for index in range(4)
                    ]
                    offsets = lax.broadcasted_iota(jnp.int32, (used * block_len, 1), 0)
                    query_pos = offsets % block_len
                    key_offsets = lax.broadcasted_iota(jnp.int32, (1, used * block_len), 1)
                    key_pos = key_offsets % block_len
                    for slot in range(used):
                        base = member_ref[cluster, slot] * block_len
                        query_pos = jnp.where(
                            offsets // block_len == slot, query_pos + base, query_pos
                        )
                        key_pos = jnp.where(
                            key_offsets // block_len == slot, key_pos + base, key_pos
                        )
                    query_pos = jnp.where(offsets // block_len < count, query_pos, -1)
                    key_pos = jnp.where(key_offsets // block_len < count, key_pos, 1 << 30)
                    computed.append((rows, count, attend_block(*tiles, query_pos, key_pos)))
                for rows, count, results in computed:
                    for slot in range(used):

                        @pl.when(slot < count)
                        def _():
                            for index in range(4):
                                out_ref[rows[slot], index] = results[index][
                                    slot * block_len : (slot + 1) * block_len
                                ].astype(out_ref.dtype)

        return carry

    lax.fori_loop(0, stride, one_step, 0)


def routed_attention(recv_table, present_count, member_table, arrived):
    smem = pl.BlockSpec(memory_space=pltpu.SMEM)
    vmem = pl.BlockSpec(memory_space=pltpu.VMEM)
    return pl.pallas_call(
        routed_kernel,
        out_shape=jax.ShapeDtypeStruct(arrived.shape, arrived.dtype),
        in_specs=[smem, smem, smem, vmem],
        out_specs=vmem,
    )(recv_table, present_count, member_table, arrived)


def pack_kernel(dest_ref, *refs):
    in_refs, out_ref = refs[:-1], refs[-1]
    head_count, block_count = dest_ref.shape
    block_len = out_ref.shape[2]
    head_dim = out_ref.shape[3]
    out_ref[...] = jnp.zeros(out_ref.shape, out_ref.dtype)
    for head in range(head_count):
        for block in range(block_count):
            slot = dest_ref[head, block]
            for index, in_ref in enumerate(in_refs):
                out_ref[slot, index] = in_ref[
                    block * block_len : (block + 1) * block_len,
                    head * head_dim : (head + 1) * head_dim,
                ]


def unpack_kernel(dest_ref, in_ref, *out_refs):
    head_count, block_count = dest_ref.shape
    block_len = in_ref.shape[2]
    head_dim = in_ref.shape[3]
    for head in range(head_count):
        for block in range(block_count):
            slot = dest_ref[head, block]
            for index, out_ref in enumerate(out_refs):
                out_ref[
                    block * block_len : (block + 1) * block_len,
                    head * head_dim : (head + 1) * head_dim,
                ] = in_ref[slot, index]


def pack_blocks(dest_table, sources, slot_count, block_len):
    smem = pl.BlockSpec(memory_space=pltpu.SMEM)
    vmem = pl.BlockSpec(memory_space=pltpu.VMEM)
    head_dim = sources[0].shape[1] // dest_table.shape[0]
    return pl.pallas_call(
        pack_kernel,
        out_shape=jax.ShapeDtypeStruct(
            (slot_count, len(sources), block_len, head_dim), sources[0].dtype
        ),
        in_specs=[smem] + [vmem] * len(sources),
        out_specs=vmem,
    )(dest_table, *sources)


def unpack_blocks(dest_table, returned, token_count):
    smem = pl.BlockSpec(memory_space=pltpu.SMEM)
    vmem = pl.BlockSpec(memory_space=pltpu.VMEM)
    width = dest_table.shape[0] * returned.shape[3]
    count = returned.shape[1]
    return pl.pallas_call(
        unpack_kernel,
        out_shape=tuple(
            jax.ShapeDtypeStruct((token_count, width), returned.dtype) for _ in range(count)
        ),
        in_specs=[smem, vmem],
        out_specs=tuple(vmem for _ in range(count)),
    )(dest_table, returned)


def per_device(queries, keys, values, cotangent, cluster_of, block_list, centroid_sums):
    seq_size = lax.axis_size("seq")
    head_count = cluster_of.shape[1]
    block_count = cluster_of.shape[2]
    token_count = queries.shape[1]
    block_len = token_count // block_count
    head_dim = centroid_sums.shape[1]
    groups_here = block_list.shape[1]
    cluster_cap = block_list.shape[2]
    owner_count = seq_size // head_count
    slot_cap = min(block_count, max(1, 2 * block_count // owner_count))
    cluster_ids = cluster_of[0]
    owner_local = cluster_ids // groups_here
    earlier = jnp.arange(block_count)[:, None] < jnp.arange(block_count)[None, :]
    same_owner = owner_local[:, :, None] == owner_local[:, None, :]
    slot_of = jnp.sum(same_owner & earlier[None], axis=1)
    dest_table = (
        owner_local * slot_cap + jnp.minimum(slot_of, slot_cap - 1)
    ).astype(jnp.int32) + (jnp.arange(head_count) * owner_count * slot_cap)[:, None].astype(jnp.int32)

    members = block_list[0].reshape(-1)
    present = members >= 0
    source_dev = jnp.where(present, members // block_count, -1)
    before = (
        present[None, :]
        & (source_dev[None, :] == source_dev[:, None])
        & (members[None, :] < members[:, None])
    )
    slot_at = jnp.sum(before, axis=1)
    recv_row = jnp.where(present, source_dev * slot_cap + slot_at, 0)

    arrived = lax.all_to_all(
        pack_blocks(
            dest_table,
            (queries[0], keys[0], values[0], cotangent[0]),
            seq_size * slot_cap,
            block_len,
        ),
        "seq",
        split_axis=0,
        concat_axis=0,
        tiled=True,
    )
    block_sums = jnp.sum(arrived[:, 1].astype(jnp.float32), axis=1)
    key_sum = jnp.sum(
        jnp.where(present[:, None], block_sums[recv_row], 0.0).reshape(
            groups_here, cluster_cap, head_dim
        ),
        axis=1,
    )
    present_count = jnp.sum(present.reshape(groups_here, cluster_cap).astype(jnp.int32), axis=1)
    outgoing = routed_attention(
        recv_row.reshape(groups_here, cluster_cap).astype(jnp.int32),
        present_count,
        jnp.where(present, members, 0).reshape(groups_here, cluster_cap).astype(jnp.int32),
        arrived,
    )
    outgoing, key_sum = lax.optimization_barrier((outgoing, key_sum))
    dp_size = lax.axis_size("dp")
    received = jnp.stack(
        [key_sum]
        + [
            lax.ppermute(
                key_sum, "dp", [(index, (index + shift) % dp_size) for index in range(dp_size)]
            )
            for shift in range(1, dp_size)
        ]
    )
    dp_index = lax.axis_index("dp")
    summed = received[dp_index % dp_size]
    for source in range(1, dp_size):
        summed = summed + received[(dp_index - source) % dp_size]
    returned = lax.all_to_all(outgoing, "seq", split_axis=0, concat_axis=0, tiled=True)
    centroid_next = decay_rate * centroid_sums + (1.0 - decay_rate) * summed
    finished = unpack_blocks(dest_table, returned, token_count)
    return tuple(item[None] for item in finished) + (centroid_next,)


def solution(mesh):
    in_specs = (
        P("dp", "seq", None),
        P("dp", "seq", None),
        P("dp", "seq", None),
        P("dp", "seq", None),
        P("dp", None, "seq"),
        P("dp", "seq", None),
        P("seq", None),
    )
    out_specs = (
        P("dp", "seq", None),
        P("dp", "seq", None),
        P("dp", "seq", None),
        P("dp", "seq", None),
        P("seq", None),
    )
    return jax.shard_map(
        per_device, mesh=mesh, in_specs=in_specs, out_specs=out_specs, check_vma=False
    )
```

```python
import math

import jax
import jax.numpy as jnp
from jax import lax
from jax.experimental import pallas as pl
from jax.experimental.pallas import tpu as pltpu
from jax.sharding import PartitionSpec as P

decay_rate = 0.99
neg_fill = -1e30


def attend_block(q, k, v, g, query_pos, key_pos):
    score_scale = 1.0 / math.sqrt(q.shape[-1])
    scores = (
        lax.dot_general(q, k, (((1,), (1,)), ((), ())), preferred_element_type=jnp.float32)
        * score_scale
    )
    visible = key_pos <= query_pos
    scores = jnp.where(visible, scores, neg_fill)
    row_max = jnp.max(scores, axis=-1, keepdims=True)
    raised = jnp.exp(scores - row_max)
    probabilities = jnp.where(visible, raised / jnp.sum(raised, axis=-1, keepdims=True), 0.0)
    weights = probabilities.astype(jnp.bfloat16)
    out_full = jnp.dot(weights, v, preferred_element_type=jnp.float32)
    dprobs = lax.dot_general(g, v, (((1,), (1,)), ((), ())), preferred_element_type=jnp.float32)
    row_dot = jnp.sum(g.astype(jnp.float32) * out_full, axis=-1, keepdims=True)
    dscores = (probabilities * (dprobs - row_dot) * score_scale).astype(jnp.bfloat16)
    grad_values = lax.dot_general(
        weights, g, (((0,), (0,)), ((), ())), preferred_element_type=jnp.float32
    )
    grad_queries = jnp.dot(dscores, k, preferred_element_type=jnp.float32)
    grad_keys = lax.dot_general(
        dscores, q, (((0,), (0,)), ((), ())), preferred_element_type=jnp.float32
    )
    return (out_full, grad_queries, grad_keys, grad_values)


def routed_kernel(recv_ref, count_ref, member_ref, arrived_ref, out_ref):
    cluster_count, cluster_cap = member_ref.shape
    block_len = arrived_ref.shape[2]

    def one_cluster(cluster, carry):
        present_count = count_ref[cluster]
        for used in range(1, cluster_cap + 1):

            @pl.when(present_count == used)
            def _():
                rows = [recv_ref[cluster, slot] for slot in range(used)]
                tiles = [
                    jnp.concatenate([arrived_ref[row, index] for row in rows], axis=0)
                    for index in range(4)
                ]
                offsets = lax.broadcasted_iota(jnp.int32, (used * block_len, 1), 0)
                query_pos = offsets % block_len
                key_offsets = lax.broadcasted_iota(jnp.int32, (1, used * block_len), 1)
                key_pos = key_offsets % block_len
                for slot in range(used):
                    base = member_ref[cluster, slot] * block_len
                    query_pos = jnp.where(offsets // block_len == slot, query_pos + base, query_pos)
                    key_pos = jnp.where(key_offsets // block_len == slot, key_pos + base, key_pos)
                results = attend_block(*tiles, query_pos, key_pos)
                for slot in range(used):
                    for index in range(4):
                        out_ref[rows[slot], index] = results[index][
                            slot * block_len : (slot + 1) * block_len
                        ].astype(out_ref.dtype)

        return carry

    lax.fori_loop(0, cluster_count, one_cluster, 0)


def routed_attention(recv_table, present_count, member_table, arrived):
    smem = pl.BlockSpec(memory_space=pltpu.SMEM)
    vmem = pl.BlockSpec(memory_space=pltpu.VMEM)
    return pl.pallas_call(
        routed_kernel,
        out_shape=jax.ShapeDtypeStruct(arrived.shape, arrived.dtype),
        in_specs=[smem, smem, smem, vmem],
        out_specs=vmem,
    )(recv_table, present_count, member_table, arrived)


def pack_kernel(dest_ref, *refs):
    in_refs, out_ref = refs[:-1], refs[-1]
    head_count, block_count = dest_ref.shape
    block_len = out_ref.shape[2]
    head_dim = out_ref.shape[3]
    for head in range(head_count):
        for block in range(block_count):
            slot = dest_ref[head, block]
            for index, in_ref in enumerate(in_refs):
                out_ref[slot, index] = in_ref[
                    block * block_len : (block + 1) * block_len,
                    head * head_dim : (head + 1) * head_dim,
                ]


def unpack_kernel(dest_ref, in_ref, *out_refs):
    head_count, block_count = dest_ref.shape
    block_len = in_ref.shape[2]
    head_dim = in_ref.shape[3]
    for head in range(head_count):
        for block in range(block_count):
            slot = dest_ref[head, block]
            for index, out_ref in enumerate(out_refs):
                out_ref[
                    block * block_len : (block + 1) * block_len,
                    head * head_dim : (head + 1) * head_dim,
                ] = in_ref[slot, index]


def pack_blocks(dest_table, sources, slot_count, block_len):
    smem = pl.BlockSpec(memory_space=pltpu.SMEM)
    vmem = pl.BlockSpec(memory_space=pltpu.VMEM)
    head_dim = sources[0].shape[1] // dest_table.shape[0]
    return pl.pallas_call(
        pack_kernel,
        out_shape=jax.ShapeDtypeStruct(
            (slot_count, len(sources), block_len, head_dim), sources[0].dtype
        ),
        in_specs=[smem] + [vmem] * len(sources),
        out_specs=vmem,
    )(dest_table, *sources)


def unpack_blocks(dest_table, returned, token_count):
    smem = pl.BlockSpec(memory_space=pltpu.SMEM)
    vmem = pl.BlockSpec(memory_space=pltpu.VMEM)
    width = dest_table.shape[0] * returned.shape[3]
    count = returned.shape[1]
    return pl.pallas_call(
        unpack_kernel,
        out_shape=tuple(
            jax.ShapeDtypeStruct((token_count, width), returned.dtype) for _ in range(count)
        ),
        in_specs=[smem, vmem],
        out_specs=tuple(vmem for _ in range(count)),
    )(dest_table, returned)


def per_device(queries, keys, values, cotangent, cluster_of, block_list, centroid_sums):
    seq_size = lax.axis_size("seq")
    head_count = cluster_of.shape[1]
    block_count = cluster_of.shape[2]
    token_count = queries.shape[1]
    block_len = token_count // block_count
    head_dim = centroid_sums.shape[1]
    groups_here = block_list.shape[1]
    cluster_cap = block_list.shape[2]
    owner_count = seq_size // head_count
    slot_cap = min(block_count, max(1, 2 * block_count // owner_count))
    cluster_ids = cluster_of[0]
    owner_local = cluster_ids // groups_here
    earlier = jnp.arange(block_count)[:, None] < jnp.arange(block_count)[None, :]
    same_owner = owner_local[:, :, None] == owner_local[:, None, :]
    slot_of = jnp.sum(same_owner & earlier[None], axis=1)
    dest_table = (
        owner_local * slot_cap + jnp.minimum(slot_of, slot_cap - 1)
    ).astype(jnp.int32) + (jnp.arange(head_count) * owner_count * slot_cap)[:, None].astype(jnp.int32)

    members = block_list[0].reshape(-1)
    present = members >= 0
    source_dev = jnp.where(present, members // block_count, -1)
    before = (
        present[None, :]
        & (source_dev[None, :] == source_dev[:, None])
        & (members[None, :] < members[:, None])
    )
    slot_at = jnp.sum(before, axis=1)
    recv_row = jnp.where(present, source_dev * slot_cap + slot_at, 0)

    arrived = lax.all_to_all(
        pack_blocks(
            dest_table,
            (queries[0], keys[0], values[0], cotangent[0]),
            seq_size * slot_cap,
            block_len,
        ),
        "seq",
        split_axis=0,
        concat_axis=0,
        tiled=True,
    )
    block_sums = jnp.sum(arrived[:, 1].astype(jnp.float32), axis=1)
    key_sum = jnp.sum(
        jnp.where(present[:, None], block_sums[recv_row], 0.0).reshape(
            groups_here, cluster_cap, head_dim
        ),
        axis=1,
    )
    present_count = jnp.sum(present.reshape(groups_here, cluster_cap).astype(jnp.int32), axis=1)
    outgoing = routed_attention(
        recv_row.reshape(groups_here, cluster_cap).astype(jnp.int32),
        present_count,
        jnp.where(present, members, 0).reshape(groups_here, cluster_cap).astype(jnp.int32),
        arrived,
    )
    outgoing, key_sum = lax.optimization_barrier((outgoing, key_sum))
    dp_size = lax.axis_size("dp")
    received = jnp.stack(
        [key_sum]
        + [
            lax.ppermute(
                key_sum, "dp", [(index, (index + shift) % dp_size) for index in range(dp_size)]
            )
            for shift in range(1, dp_size)
        ]
    )
    dp_index = lax.axis_index("dp")
    summed = received[dp_index % dp_size]
    for source in range(1, dp_size):
        summed = summed + received[(dp_index - source) % dp_size]
    returned = lax.all_to_all(outgoing, "seq", split_axis=0, concat_axis=0, tiled=True)
    centroid_next = decay_rate * centroid_sums + (1.0 - decay_rate) * summed
    finished = unpack_blocks(dest_table, returned, token_count)
    return tuple(item[None] for item in finished) + (centroid_next,)


def solution(mesh):
    in_specs = (
        P("dp", "seq", None),
        P("dp", "seq", None),
        P("dp", "seq", None),
        P("dp", "seq", None),
        P("dp", None, "seq"),
        P("dp", "seq", None),
        P("seq", None),
    )
    out_specs = (
        P("dp", "seq", None),
        P("dp", "seq", None),
        P("dp", "seq", None),
        P("dp", "seq", None),
        P("seq", None),
    )
    return jax.shard_map(
        per_device, mesh=mesh, in_specs=in_specs, out_specs=out_specs, check_vma=False
    )
```

```python
import math

import jax
import jax.numpy as jnp
from jax import lax
from jax.experimental import pallas as pl
from jax.experimental.pallas import tpu as pltpu
from jax.sharding import PartitionSpec as P

decay_rate = 0.99
neg_fill = -1e30


def attend_block(q, k, v, g, query_pos, key_pos):
    score_scale = 1.0 / math.sqrt(q.shape[-1])
    scores = (
        lax.dot_general(q, k, (((1,), (1,)), ((), ())), preferred_element_type=jnp.float32)
        * score_scale
    )
    visible = key_pos <= query_pos
    scores = jnp.where(visible, scores, neg_fill)
    row_max = jnp.max(scores, axis=-1, keepdims=True)
    raised = jnp.exp(scores - row_max)
    probabilities = jnp.where(visible, raised / jnp.sum(raised, axis=-1, keepdims=True), 0.0)
    weights = probabilities.astype(jnp.bfloat16)
    out_full = jnp.dot(weights, v, preferred_element_type=jnp.float32)
    dprobs = lax.dot_general(g, v, (((1,), (1,)), ((), ())), preferred_element_type=jnp.float32)
    row_dot = jnp.sum(g.astype(jnp.float32) * out_full, axis=-1, keepdims=True)
    dscores = (probabilities * (dprobs - row_dot) * score_scale).astype(jnp.bfloat16)
    grad_values = lax.dot_general(
        weights, g, (((0,), (0,)), ((), ())), preferred_element_type=jnp.float32
    )
    grad_queries = jnp.dot(dscores, k, preferred_element_type=jnp.float32)
    grad_keys = lax.dot_general(
        dscores, q, (((0,), (0,)), ((), ())), preferred_element_type=jnp.float32
    )
    return (out_full, grad_queries, grad_keys, grad_values)


def routed_kernel(recv_ref, count_ref, member_ref, arrived_ref, out_ref):
    cluster_count, cluster_cap = member_ref.shape
    block_len = arrived_ref.shape[2]

    def one_cluster(cluster, carry):
        present_count = count_ref[cluster]
        for used in range(1, cluster_cap + 1):

            @pl.when(present_count == used)
            def _():
                rows = [recv_ref[cluster, slot] for slot in range(used)]
                tiles = [
                    jnp.concatenate([arrived_ref[row, index] for row in rows], axis=0)
                    for index in range(4)
                ]
                offsets = lax.broadcasted_iota(jnp.int32, (used * block_len, 1), 0)
                query_pos = offsets % block_len
                key_offsets = lax.broadcasted_iota(jnp.int32, (1, used * block_len), 1)
                key_pos = key_offsets % block_len
                for slot in range(used):
                    base = member_ref[cluster, slot] * block_len
                    query_pos = jnp.where(offsets // block_len == slot, query_pos + base, query_pos)
                    key_pos = jnp.where(key_offsets // block_len == slot, key_pos + base, key_pos)
                results = attend_block(*tiles, query_pos, key_pos)
                for slot in range(used):
                    for index in range(4):
                        out_ref[rows[slot], index] = results[index][
                            slot * block_len : (slot + 1) * block_len
                        ].astype(out_ref.dtype)

        return carry

    lax.fori_loop(0, cluster_count, one_cluster, 0)


def routed_attention(recv_table, present_count, member_table, arrived):
    smem = pl.BlockSpec(memory_space=pltpu.SMEM)
    vmem = pl.BlockSpec(memory_space=pltpu.VMEM)
    return pl.pallas_call(
        routed_kernel,
        out_shape=jax.ShapeDtypeStruct(arrived.shape, arrived.dtype),
        in_specs=[smem, smem, smem, vmem],
        out_specs=vmem,
    )(recv_table, present_count, member_table, arrived)


def pack_kernel(dest_ref, *refs):
    in_refs, out_ref, sems = refs[:-2], refs[-2], refs[-1]
    head_count, block_count = dest_ref.shape
    block_len = out_ref.shape[2]
    head_dim = out_ref.shape[3]
    copies = []
    for head in range(head_count):
        for block in range(block_count):
            slot = dest_ref[head, block]
            for index, in_ref in enumerate(in_refs):
                copy = pltpu.make_async_copy(
                    in_ref.at[
                        pl.ds(block * block_len, block_len), pl.ds(head * head_dim, head_dim)
                    ],
                    out_ref.at[slot, index],
                    sems.at[len(copies)],
                )
                copy.start()
                copies.append(copy)
    for copy in copies:
        copy.wait()


def unpack_kernel(dest_ref, in_ref, *refs):
    out_refs, sems = refs[:-1], refs[-1]
    head_count, block_count = dest_ref.shape
    block_len = in_ref.shape[2]
    head_dim = in_ref.shape[3]
    copies = []
    for head in range(head_count):
        for block in range(block_count):
            slot = dest_ref[head, block]
            for index, out_ref in enumerate(out_refs):
                copy = pltpu.make_async_copy(
                    in_ref.at[slot, index],
                    out_ref.at[
                        pl.ds(block * block_len, block_len), pl.ds(head * head_dim, head_dim)
                    ],
                    sems.at[len(copies)],
                )
                copy.start()
                copies.append(copy)
    for copy in copies:
        copy.wait()


def pack_blocks(dest_table, sources, slot_count, block_len):
    smem = pl.BlockSpec(memory_space=pltpu.SMEM)
    anywhere = pl.BlockSpec(memory_space=pl.ANY)
    head_dim = sources[0].shape[1] // dest_table.shape[0]
    return pl.pallas_call(
        pack_kernel,
        out_shape=jax.ShapeDtypeStruct(
            (slot_count, len(sources), block_len, head_dim), sources[0].dtype
        ),
        in_specs=[smem] + [anywhere] * len(sources),
        out_specs=anywhere,
        scratch_shapes=[pltpu.SemaphoreType.DMA((dest_table.size * len(sources),))],
    )(dest_table, *sources)


def unpack_blocks(dest_table, returned, token_count):
    smem = pl.BlockSpec(memory_space=pltpu.SMEM)
    anywhere = pl.BlockSpec(memory_space=pl.ANY)
    width = dest_table.shape[0] * returned.shape[3]
    count = returned.shape[1]
    return pl.pallas_call(
        unpack_kernel,
        out_shape=tuple(
            jax.ShapeDtypeStruct((token_count, width), returned.dtype) for _ in range(count)
        ),
        in_specs=[smem, anywhere],
        out_specs=tuple(anywhere for _ in range(count)),
        scratch_shapes=[pltpu.SemaphoreType.DMA((dest_table.size * count,))],
    )(dest_table, returned)


def per_device(queries, keys, values, cotangent, cluster_of, block_list, centroid_sums):
    seq_size = lax.axis_size("seq")
    head_count = cluster_of.shape[1]
    block_count = cluster_of.shape[2]
    token_count = queries.shape[1]
    block_len = token_count // block_count
    head_dim = centroid_sums.shape[1]
    groups_here = block_list.shape[1]
    cluster_cap = block_list.shape[2]
    owner_count = seq_size // head_count
    slot_cap = min(block_count, max(1, 2 * block_count // owner_count))
    cluster_ids = cluster_of[0]
    owner_local = cluster_ids // groups_here
    earlier = jnp.arange(block_count)[:, None] < jnp.arange(block_count)[None, :]
    same_owner = owner_local[:, :, None] == owner_local[:, None, :]
    slot_of = jnp.sum(same_owner & earlier[None], axis=1)
    dest_table = (
        owner_local * slot_cap + jnp.minimum(slot_of, slot_cap - 1)
    ).astype(jnp.int32) + (jnp.arange(head_count) * owner_count * slot_cap)[:, None].astype(jnp.int32)

    members = block_list[0].reshape(-1)
    present = members >= 0
    source_dev = jnp.where(present, members // block_count, -1)
    before = (
        present[None, :]
        & (source_dev[None, :] == source_dev[:, None])
        & (members[None, :] < members[:, None])
    )
    slot_at = jnp.sum(before, axis=1)
    recv_row = jnp.where(present, source_dev * slot_cap + slot_at, 0)

    arrived = lax.all_to_all(
        pack_blocks(
            dest_table,
            (queries[0], keys[0], values[0], cotangent[0]),
            seq_size * slot_cap,
            block_len,
        ),
        "seq",
        split_axis=0,
        concat_axis=0,
        tiled=True,
    )
    block_sums = jnp.sum(arrived[:, 1].astype(jnp.float32), axis=1)
    key_sum = jnp.sum(
        jnp.where(present[:, None], block_sums[recv_row], 0.0).reshape(
            groups_here, cluster_cap, head_dim
        ),
        axis=1,
    )
    present_count = jnp.sum(present.reshape(groups_here, cluster_cap).astype(jnp.int32), axis=1)
    outgoing = routed_attention(
        recv_row.reshape(groups_here, cluster_cap).astype(jnp.int32),
        present_count,
        jnp.where(present, members, 0).reshape(groups_here, cluster_cap).astype(jnp.int32),
        arrived,
    )
    outgoing, key_sum = lax.optimization_barrier((outgoing, key_sum))
    dp_size = lax.axis_size("dp")
    received = jnp.stack(
        [key_sum]
        + [
            lax.ppermute(
                key_sum, "dp", [(index, (index + shift) % dp_size) for index in range(dp_size)]
            )
            for shift in range(1, dp_size)
        ]
    )
    dp_index = lax.axis_index("dp")
    summed = received[dp_index % dp_size]
    for source in range(1, dp_size):
        summed = summed + received[(dp_index - source) % dp_size]
    returned = lax.all_to_all(outgoing, "seq", split_axis=0, concat_axis=0, tiled=True)
    centroid_next = decay_rate * centroid_sums + (1.0 - decay_rate) * summed
    finished = unpack_blocks(dest_table, returned, token_count)
    return tuple(item[None] for item in finished) + (centroid_next,)


def solution(mesh):
    in_specs = (
        P("dp", "seq", None),
        P("dp", "seq", None),
        P("dp", "seq", None),
        P("dp", "seq", None),
        P("dp", None, "seq"),
        P("dp", "seq", None),
        P("seq", None),
    )
    out_specs = (
        P("dp", "seq", None),
        P("dp", "seq", None),
        P("dp", "seq", None),
        P("dp", "seq", None),
        P("seq", None),
    )
    return jax.shard_map(
        per_device, mesh=mesh, in_specs=in_specs, out_specs=out_specs, check_vma=False
    )
```

```python
import math

import jax
import jax.numpy as jnp
from jax import lax
from jax.experimental import pallas as pl
from jax.experimental.pallas import tpu as pltpu
from jax.sharding import PartitionSpec as P

decay_rate = 0.99
neg_fill = -1e30


def attend_block(q, k, v, g, query_pos, key_pos):
    score_scale = 1.0 / math.sqrt(q.shape[-1])
    scores = (
        lax.dot_general(q, k, (((1,), (1,)), ((), ())), preferred_element_type=jnp.float32)
        * score_scale
    )
    visible = key_pos <= query_pos
    scores = jnp.where(visible, scores, neg_fill)
    row_max = jnp.max(scores, axis=-1, keepdims=True)
    raised = jnp.exp(scores - row_max)
    probabilities = jnp.where(visible, raised / jnp.sum(raised, axis=-1, keepdims=True), 0.0)
    weights = probabilities.astype(jnp.bfloat16)
    out_full = jnp.dot(weights, v, preferred_element_type=jnp.float32)
    dprobs = lax.dot_general(g, v, (((1,), (1,)), ((), ())), preferred_element_type=jnp.float32)
    row_dot = jnp.sum(g.astype(jnp.float32) * out_full, axis=-1, keepdims=True)
    dscores = (probabilities * (dprobs - row_dot) * score_scale).astype(jnp.bfloat16)
    grad_values = lax.dot_general(
        weights, g, (((0,), (0,)), ((), ())), preferred_element_type=jnp.float32
    )
    grad_queries = jnp.dot(dscores, k, preferred_element_type=jnp.float32)
    grad_keys = lax.dot_general(
        dscores, q, (((0,), (0,)), ((), ())), preferred_element_type=jnp.float32
    )
    return (out_full, grad_queries, grad_keys, grad_values)


def routed_kernel(recv_ref, count_ref, member_ref, arrived_ref, out_ref, sums_ref):
    cluster_count, cluster_cap = member_ref.shape
    block_len = arrived_ref.shape[2]

    sums_ref[...] = jnp.zeros(sums_ref.shape, sums_ref.dtype)

    def one_cluster(cluster, carry):
        present_count = count_ref[cluster]
        for used in range(1, cluster_cap + 1):

            @pl.when(present_count == used)
            def _():
                rows = [recv_ref[cluster, slot] for slot in range(used)]
                tiles = [
                    jnp.concatenate([arrived_ref[row, index] for row in rows], axis=0)
                    for index in range(4)
                ]
                offsets = lax.broadcasted_iota(jnp.int32, (used * block_len, 1), 0)
                query_pos = offsets % block_len
                key_offsets = lax.broadcasted_iota(jnp.int32, (1, used * block_len), 1)
                key_pos = key_offsets % block_len
                for slot in range(used):
                    base = member_ref[cluster, slot] * block_len
                    query_pos = jnp.where(offsets // block_len == slot, query_pos + base, query_pos)
                    key_pos = jnp.where(key_offsets // block_len == slot, key_pos + base, key_pos)
                results = attend_block(*tiles, query_pos, key_pos)
                key_total = jnp.sum(tiles[1].astype(jnp.float32), axis=0, keepdims=True)
                sums_ref[cluster] = jnp.broadcast_to(key_total, sums_ref.shape[1:])
                for slot in range(used):
                    for index in range(4):
                        out_ref[rows[slot], index] = results[index][
                            slot * block_len : (slot + 1) * block_len
                        ].astype(out_ref.dtype)

        return carry

    lax.fori_loop(0, cluster_count, one_cluster, 0)


def routed_attention(recv_table, present_count, member_table, arrived):
    smem = pl.BlockSpec(memory_space=pltpu.SMEM)
    vmem = pl.BlockSpec(memory_space=pltpu.VMEM)
    return pl.pallas_call(
        routed_kernel,
        out_shape=(
            jax.ShapeDtypeStruct(arrived.shape, arrived.dtype),
            jax.ShapeDtypeStruct((member_table.shape[0], 8, arrived.shape[3]), jnp.float32),
        ),
        in_specs=[smem, smem, smem, vmem],
        out_specs=(vmem, vmem),
    )(recv_table, present_count, member_table, arrived)


def pack_kernel(dest_ref, *refs):
    in_refs, out_ref = refs[:-1], refs[-1]
    head_count, block_count = dest_ref.shape
    block_len = out_ref.shape[2]
    head_dim = out_ref.shape[3]
    for head in range(head_count):
        for block in range(block_count):
            slot = dest_ref[head, block]
            for index, in_ref in enumerate(in_refs):
                out_ref[slot, index] = in_ref[
                    block * block_len : (block + 1) * block_len,
                    head * head_dim : (head + 1) * head_dim,
                ]


def unpack_kernel(dest_ref, in_ref, *out_refs):
    head_count, block_count = dest_ref.shape
    block_len = in_ref.shape[2]
    head_dim = in_ref.shape[3]
    for head in range(head_count):
        for block in range(block_count):
            slot = dest_ref[head, block]
            for index, out_ref in enumerate(out_refs):
                out_ref[
                    block * block_len : (block + 1) * block_len,
                    head * head_dim : (head + 1) * head_dim,
                ] = in_ref[slot, index]


def pack_blocks(dest_table, sources, slot_count, block_len):
    smem = pl.BlockSpec(memory_space=pltpu.SMEM)
    vmem = pl.BlockSpec(memory_space=pltpu.VMEM)
    head_dim = sources[0].shape[1] // dest_table.shape[0]
    return pl.pallas_call(
        pack_kernel,
        out_shape=jax.ShapeDtypeStruct(
            (slot_count, len(sources), block_len, head_dim), sources[0].dtype
        ),
        in_specs=[smem] + [vmem] * len(sources),
        out_specs=vmem,
    )(dest_table, *sources)


def unpack_blocks(dest_table, returned, token_count):
    smem = pl.BlockSpec(memory_space=pltpu.SMEM)
    vmem = pl.BlockSpec(memory_space=pltpu.VMEM)
    width = dest_table.shape[0] * returned.shape[3]
    count = returned.shape[1]
    return pl.pallas_call(
        unpack_kernel,
        out_shape=tuple(
            jax.ShapeDtypeStruct((token_count, width), returned.dtype) for _ in range(count)
        ),
        in_specs=[smem, vmem],
        out_specs=tuple(vmem for _ in range(count)),
    )(dest_table, returned)


def per_device(queries, keys, values, cotangent, cluster_of, block_list, centroid_sums):
    seq_size = lax.axis_size("seq")
    head_count = cluster_of.shape[1]
    block_count = cluster_of.shape[2]
    token_count = queries.shape[1]
    block_len = token_count // block_count
    head_dim = centroid_sums.shape[1]
    groups_here = block_list.shape[1]
    cluster_cap = block_list.shape[2]
    owner_count = seq_size // head_count
    slot_cap = min(block_count, max(1, 2 * block_count // owner_count))
    cluster_ids = cluster_of[0]
    owner_local = cluster_ids // groups_here
    earlier = jnp.arange(block_count)[:, None] < jnp.arange(block_count)[None, :]
    same_owner = owner_local[:, :, None] == owner_local[:, None, :]
    slot_of = jnp.sum(same_owner & earlier[None], axis=1)
    dest_table = (
        owner_local * slot_cap + jnp.minimum(slot_of, slot_cap - 1)
    ).astype(jnp.int32) + (jnp.arange(head_count) * owner_count * slot_cap)[:, None].astype(jnp.int32)

    members = block_list[0].reshape(-1)
    present = members >= 0
    source_dev = jnp.where(present, members // block_count, -1)
    before = (
        present[None, :]
        & (source_dev[None, :] == source_dev[:, None])
        & (members[None, :] < members[:, None])
    )
    slot_at = jnp.sum(before, axis=1)
    recv_row = jnp.where(present, source_dev * slot_cap + slot_at, 0)

    arrived = lax.all_to_all(
        pack_blocks(
            dest_table,
            (queries[0], keys[0], values[0], cotangent[0]),
            seq_size * slot_cap,
            block_len,
        ),
        "seq",
        split_axis=0,
        concat_axis=0,
        tiled=True,
    )
    present_count = jnp.sum(present.reshape(groups_here, cluster_cap).astype(jnp.int32), axis=1)
    outgoing, key_sums = routed_attention(
        recv_row.reshape(groups_here, cluster_cap).astype(jnp.int32),
        present_count,
        jnp.where(present, members, 0).reshape(groups_here, cluster_cap).astype(jnp.int32),
        arrived,
    )
    key_sum = key_sums[:, 0]
    dp_size = lax.axis_size("dp")
    received = jnp.stack(
        [key_sum]
        + [
            lax.ppermute(
                key_sum, "dp", [(index, (index + shift) % dp_size) for index in range(dp_size)]
            )
            for shift in range(1, dp_size)
        ]
    )
    dp_index = lax.axis_index("dp")
    summed = received[dp_index % dp_size]
    for source in range(1, dp_size):
        summed = summed + received[(dp_index - source) % dp_size]
    returned = lax.all_to_all(outgoing, "seq", split_axis=0, concat_axis=0, tiled=True)
    centroid_next = decay_rate * centroid_sums + (1.0 - decay_rate) * summed
    finished = unpack_blocks(dest_table, returned, token_count)
    return tuple(item[None] for item in finished) + (centroid_next,)


def solution(mesh):
    in_specs = (
        P("dp", "seq", None),
        P("dp", "seq", None),
        P("dp", "seq", None),
        P("dp", "seq", None),
        P("dp", None, "seq"),
        P("dp", "seq", None),
        P("seq", None),
    )
    out_specs = (
        P("dp", "seq", None),
        P("dp", "seq", None),
        P("dp", "seq", None),
        P("dp", "seq", None),
        P("seq", None),
    )
    return jax.shard_map(
        per_device, mesh=mesh, in_specs=in_specs, out_specs=out_specs, check_vma=False
    )
```

```python
import math

import jax
import jax.numpy as jnp
from jax import lax
from jax.experimental import pallas as pl
from jax.experimental.pallas import tpu as pltpu
from jax.sharding import PartitionSpec as P

decay_rate = 0.99
neg_fill = -1e30


def attend_block(q, k, v, g, query_pos, key_pos):
    score_scale = 1.0 / math.sqrt(q.shape[-1])
    scores = (
        lax.dot_general(q, k, (((1,), (1,)), ((), ())), preferred_element_type=jnp.float32)
        * score_scale
    )
    visible = key_pos <= query_pos
    scores = jnp.where(visible, scores, neg_fill)
    row_max = jnp.max(scores, axis=-1, keepdims=True)
    raised = jnp.exp(scores - row_max)
    probabilities = jnp.where(visible, raised / jnp.sum(raised, axis=-1, keepdims=True), 0.0)
    weights = probabilities.astype(jnp.bfloat16)
    out_full = jnp.dot(weights, v, preferred_element_type=jnp.float32)
    dprobs = lax.dot_general(g, v, (((1,), (1,)), ((), ())), preferred_element_type=jnp.float32)
    row_dot = jnp.sum(g.astype(jnp.float32) * out_full, axis=-1, keepdims=True)
    dscores = (probabilities * (dprobs - row_dot) * score_scale).astype(jnp.bfloat16)
    grad_values = lax.dot_general(
        weights, g, (((0,), (0,)), ((), ())), preferred_element_type=jnp.float32
    )
    grad_queries = jnp.dot(dscores, k, preferred_element_type=jnp.float32)
    grad_keys = lax.dot_general(
        dscores, q, (((0,), (0,)), ((), ())), preferred_element_type=jnp.float32
    )
    return (out_full, grad_queries, grad_keys, grad_values)


def routed_kernel(recv_ref, count_ref, member_ref, arrived_ref, out_ref):
    cluster_count, cluster_cap = member_ref.shape
    block_len = arrived_ref.shape[2]

    def one_cluster(cluster, carry):
        present_count = count_ref[cluster]
        for used in range(1, cluster_cap + 1):

            @pl.when(present_count == used)
            def _():
                rows = [recv_ref[cluster, slot] for slot in range(used)]
                tiles = [
                    jnp.concatenate([arrived_ref[row, index] for row in rows], axis=0)
                    for index in range(4)
                ]
                offsets = lax.broadcasted_iota(jnp.int32, (used * block_len, 1), 0)
                query_pos = offsets % block_len
                key_offsets = lax.broadcasted_iota(jnp.int32, (1, used * block_len), 1)
                key_pos = key_offsets % block_len
                for slot in range(used):
                    base = member_ref[cluster, slot] * block_len
                    query_pos = jnp.where(offsets // block_len == slot, query_pos + base, query_pos)
                    key_pos = jnp.where(key_offsets // block_len == slot, key_pos + base, key_pos)
                results = attend_block(*tiles, query_pos, key_pos)
                for slot in range(used):
                    for index in range(4):
                        out_ref[rows[slot], index] = results[index][
                            slot * block_len : (slot + 1) * block_len
                        ].astype(out_ref.dtype)

        return carry

    lax.fori_loop(0, cluster_count, one_cluster, 0, unroll=2)


def routed_attention(recv_table, present_count, member_table, arrived):
    smem = pl.BlockSpec(memory_space=pltpu.SMEM)
    vmem = pl.BlockSpec(memory_space=pltpu.VMEM)
    return pl.pallas_call(
        routed_kernel,
        out_shape=jax.ShapeDtypeStruct(arrived.shape, arrived.dtype),
        in_specs=[smem, smem, smem, vmem],
        out_specs=vmem,
    )(recv_table, present_count, member_table, arrived)


def pack_kernel(dest_ref, *refs):
    in_refs, out_ref = refs[:-1], refs[-1]
    head_count, block_count = dest_ref.shape
    block_len = out_ref.shape[2]
    head_dim = out_ref.shape[3]
    for head in range(head_count):
        for block in range(block_count):
            slot = dest_ref[head, block]
            for index, in_ref in enumerate(in_refs):
                out_ref[slot, index] = in_ref[
                    block * block_len : (block + 1) * block_len,
                    head * head_dim : (head + 1) * head_dim,
                ]


def unpack_kernel(dest_ref, in_ref, *out_refs):
    head_count, block_count = dest_ref.shape
    block_len = in_ref.shape[2]
    head_dim = in_ref.shape[3]
    for head in range(head_count):
        for block in range(block_count):
            slot = dest_ref[head, block]
            for index, out_ref in enumerate(out_refs):
                out_ref[
                    block * block_len : (block + 1) * block_len,
                    head * head_dim : (head + 1) * head_dim,
                ] = in_ref[slot, index]


def pack_blocks(dest_table, sources, slot_count, block_len):
    smem = pl.BlockSpec(memory_space=pltpu.SMEM)
    vmem = pl.BlockSpec(memory_space=pltpu.VMEM)
    head_dim = sources[0].shape[1] // dest_table.shape[0]
    return pl.pallas_call(
        pack_kernel,
        out_shape=jax.ShapeDtypeStruct(
            (slot_count, len(sources), block_len, head_dim), sources[0].dtype
        ),
        in_specs=[smem] + [vmem] * len(sources),
        out_specs=vmem,
    )(dest_table, *sources)


def unpack_blocks(dest_table, returned, token_count):
    smem = pl.BlockSpec(memory_space=pltpu.SMEM)
    vmem = pl.BlockSpec(memory_space=pltpu.VMEM)
    width = dest_table.shape[0] * returned.shape[3]
    count = returned.shape[1]
    return pl.pallas_call(
        unpack_kernel,
        out_shape=tuple(
            jax.ShapeDtypeStruct((token_count, width), returned.dtype) for _ in range(count)
        ),
        in_specs=[smem, vmem],
        out_specs=tuple(vmem for _ in range(count)),
    )(dest_table, returned)


def per_device(queries, keys, values, cotangent, cluster_of, block_list, centroid_sums):
    seq_size = lax.axis_size("seq")
    head_count = cluster_of.shape[1]
    block_count = cluster_of.shape[2]
    token_count = queries.shape[1]
    block_len = token_count // block_count
    head_dim = centroid_sums.shape[1]
    groups_here = block_list.shape[1]
    cluster_cap = block_list.shape[2]
    owner_count = seq_size // head_count
    slot_cap = min(block_count, max(1, 2 * block_count // owner_count))
    cluster_ids = cluster_of[0]
    owner_local = cluster_ids // groups_here
    earlier = jnp.arange(block_count)[:, None] < jnp.arange(block_count)[None, :]
    same_owner = owner_local[:, :, None] == owner_local[:, None, :]
    slot_of = jnp.sum(same_owner & earlier[None], axis=1)
    dest_table = (
        owner_local * slot_cap + jnp.minimum(slot_of, slot_cap - 1)
    ).astype(jnp.int32) + (jnp.arange(head_count) * owner_count * slot_cap)[:, None].astype(jnp.int32)

    members = block_list[0].reshape(-1)
    present = members >= 0
    source_dev = jnp.where(present, members // block_count, -1)
    before = (
        present[None, :]
        & (source_dev[None, :] == source_dev[:, None])
        & (members[None, :] < members[:, None])
    )
    slot_at = jnp.sum(before, axis=1)
    recv_row = jnp.where(present, source_dev * slot_cap + slot_at, 0)

    arrived = lax.all_to_all(
        pack_blocks(
            dest_table,
            (queries[0], keys[0], values[0], cotangent[0]),
            seq_size * slot_cap,
            block_len,
        ),
        "seq",
        split_axis=0,
        concat_axis=0,
        tiled=True,
    )
    block_sums = jnp.sum(arrived[:, 1].astype(jnp.float32), axis=1)
    key_sum = jnp.sum(
        jnp.where(present[:, None], block_sums[recv_row], 0.0).reshape(
            groups_here, cluster_cap, head_dim
        ),
        axis=1,
    )
    present_count = jnp.sum(present.reshape(groups_here, cluster_cap).astype(jnp.int32), axis=1)
    outgoing = routed_attention(
        recv_row.reshape(groups_here, cluster_cap).astype(jnp.int32),
        present_count,
        jnp.where(present, members, 0).reshape(groups_here, cluster_cap).astype(jnp.int32),
        arrived,
    )
    outgoing, key_sum = lax.optimization_barrier((outgoing, key_sum))
    dp_size = lax.axis_size("dp")
    received = jnp.stack(
        [key_sum]
        + [
            lax.ppermute(
                key_sum, "dp", [(index, (index + shift) % dp_size) for index in range(dp_size)]
            )
            for shift in range(1, dp_size)
        ]
    )
    dp_index = lax.axis_index("dp")
    summed = received[dp_index % dp_size]
    for source in range(1, dp_size):
        summed = summed + received[(dp_index - source) % dp_size]
    returned = lax.all_to_all(outgoing, "seq", split_axis=0, concat_axis=0, tiled=True)
    centroid_next = decay_rate * centroid_sums + (1.0 - decay_rate) * summed
    finished = unpack_blocks(dest_table, returned, token_count)
    return tuple(item[None] for item in finished) + (centroid_next,)


def solution(mesh):
    in_specs = (
        P("dp", "seq", None),
        P("dp", "seq", None),
        P("dp", "seq", None),
        P("dp", "seq", None),
        P("dp", None, "seq"),
        P("dp", "seq", None),
        P("seq", None),
    )
    out_specs = (
        P("dp", "seq", None),
        P("dp", "seq", None),
        P("dp", "seq", None),
        P("dp", "seq", None),
        P("seq", None),
    )
    return jax.shard_map(
        per_device, mesh=mesh, in_specs=in_specs, out_specs=out_specs, check_vma=False
    )
```

```python
import math

import jax
import jax.numpy as jnp
from jax import lax
from jax.experimental import pallas as pl
from jax.experimental.pallas import tpu as pltpu
from jax.sharding import PartitionSpec as P

decay_rate = 0.99
neg_fill = -1e30


def attend_block(q, k, v, g, query_pos, key_pos):
    score_scale = 1.0 / math.sqrt(q.shape[-1])
    scores = (
        lax.dot_general(q, k, (((1,), (1,)), ((), ())), preferred_element_type=jnp.float32)
        * score_scale
    )
    visible = key_pos <= query_pos
    scores = jnp.where(visible, scores, neg_fill)
    row_max = jnp.max(scores, axis=-1, keepdims=True)
    raised = jnp.exp(scores - row_max)
    probabilities = jnp.where(visible, raised / jnp.sum(raised, axis=-1, keepdims=True), 0.0)
    weights = probabilities.astype(jnp.bfloat16)
    out_full = jnp.dot(weights, v, preferred_element_type=jnp.float32)
    dprobs = lax.dot_general(g, v, (((1,), (1,)), ((), ())), preferred_element_type=jnp.float32)
    row_dot = jnp.sum(g.astype(jnp.float32) * out_full, axis=-1, keepdims=True)
    dscores = (probabilities * (dprobs - row_dot) * score_scale).astype(jnp.bfloat16)
    grad_values = lax.dot_general(
        weights, g, (((0,), (0,)), ((), ())), preferred_element_type=jnp.float32
    )
    grad_queries = jnp.dot(dscores, k, preferred_element_type=jnp.float32)
    grad_keys = lax.dot_general(
        dscores, q, (((0,), (0,)), ((), ())), preferred_element_type=jnp.float32
    )
    return (out_full, grad_queries, grad_keys, grad_values)


def routed_kernel(recv_ref, count_ref, member_ref, arrived_ref, out_ref):
    cluster_count, cluster_cap = member_ref.shape
    block_len = arrived_ref.shape[2]

    def one_cluster(cluster, carry):
        present_count = count_ref[cluster]
        for used in range(1, cluster_cap + 1):

            @pl.when(present_count == used)
            def _():
                rows = [recv_ref[cluster, slot] for slot in range(used)]
                tiles = [
                    jnp.concatenate([arrived_ref[row, index] for row in rows], axis=0)
                    for index in range(4)
                ]
                offsets = lax.broadcasted_iota(jnp.int32, (used * block_len, 1), 0)
                query_pos = offsets % block_len
                key_offsets = lax.broadcasted_iota(jnp.int32, (1, used * block_len), 1)
                key_pos = key_offsets % block_len
                for slot in range(used):
                    base = member_ref[cluster, slot] * block_len
                    query_pos = jnp.where(offsets // block_len == slot, query_pos + base, query_pos)
                    key_pos = jnp.where(key_offsets // block_len == slot, key_pos + base, key_pos)
                results = attend_block(*tiles, query_pos, key_pos)
                for slot in range(used):
                    for index in range(4):
                        out_ref[rows[slot], index] = results[index][
                            slot * block_len : (slot + 1) * block_len
                        ].astype(out_ref.dtype)

        return carry

    lax.fori_loop(0, cluster_count, one_cluster, 0, unroll=4)


def routed_attention(recv_table, present_count, member_table, arrived):
    smem = pl.BlockSpec(memory_space=pltpu.SMEM)
    vmem = pl.BlockSpec(memory_space=pltpu.VMEM)
    return pl.pallas_call(
        routed_kernel,
        out_shape=jax.ShapeDtypeStruct(arrived.shape, arrived.dtype),
        in_specs=[smem, smem, smem, vmem],
        out_specs=vmem,
    )(recv_table, present_count, member_table, arrived)


def pack_kernel(dest_ref, *refs):
    in_refs, out_ref = refs[:-1], refs[-1]
    head_count, block_count = dest_ref.shape
    block_len = out_ref.shape[2]
    head_dim = out_ref.shape[3]
    for head in range(head_count):
        for block in range(block_count):
            slot = dest_ref[head, block]
            for index, in_ref in enumerate(in_refs):
                out_ref[slot, index] = in_ref[
                    block * block_len : (block + 1) * block_len,
                    head * head_dim : (head + 1) * head_dim,
                ]


def unpack_kernel(dest_ref, in_ref, *out_refs):
    head_count, block_count = dest_ref.shape
    block_len = in_ref.shape[2]
    head_dim = in_ref.shape[3]
    for head in range(head_count):
        for block in range(block_count):
            slot = dest_ref[head, block]
            for index, out_ref in enumerate(out_refs):
                out_ref[
                    block * block_len : (block + 1) * block_len,
                    head * head_dim : (head + 1) * head_dim,
                ] = in_ref[slot, index]


def pack_blocks(dest_table, sources, slot_count, block_len):
    smem = pl.BlockSpec(memory_space=pltpu.SMEM)
    vmem = pl.BlockSpec(memory_space=pltpu.VMEM)
    head_dim = sources[0].shape[1] // dest_table.shape[0]
    return pl.pallas_call(
        pack_kernel,
        out_shape=jax.ShapeDtypeStruct(
            (slot_count, len(sources), block_len, head_dim), sources[0].dtype
        ),
        in_specs=[smem] + [vmem] * len(sources),
        out_specs=vmem,
    )(dest_table, *sources)


def unpack_blocks(dest_table, returned, token_count):
    smem = pl.BlockSpec(memory_space=pltpu.SMEM)
    vmem = pl.BlockSpec(memory_space=pltpu.VMEM)
    width = dest_table.shape[0] * returned.shape[3]
    count = returned.shape[1]
    return pl.pallas_call(
        unpack_kernel,
        out_shape=tuple(
            jax.ShapeDtypeStruct((token_count, width), returned.dtype) for _ in range(count)
        ),
        in_specs=[smem, vmem],
        out_specs=tuple(vmem for _ in range(count)),
    )(dest_table, returned)


def per_device(queries, keys, values, cotangent, cluster_of, block_list, centroid_sums):
    seq_size = lax.axis_size("seq")
    head_count = cluster_of.shape[1]
    block_count = cluster_of.shape[2]
    token_count = queries.shape[1]
    block_len = token_count // block_count
    head_dim = centroid_sums.shape[1]
    groups_here = block_list.shape[1]
    cluster_cap = block_list.shape[2]
    owner_count = seq_size // head_count
    slot_cap = min(block_count, max(1, 2 * block_count // owner_count))
    cluster_ids = cluster_of[0]
    owner_local = cluster_ids // groups_here
    earlier = jnp.arange(block_count)[:, None] < jnp.arange(block_count)[None, :]
    same_owner = owner_local[:, :, None] == owner_local[:, None, :]
    slot_of = jnp.sum(same_owner & earlier[None], axis=1)
    dest_table = (
        owner_local * slot_cap + jnp.minimum(slot_of, slot_cap - 1)
    ).astype(jnp.int32) + (jnp.arange(head_count) * owner_count * slot_cap)[:, None].astype(jnp.int32)

    members = block_list[0].reshape(-1)
    present = members >= 0
    source_dev = jnp.where(present, members // block_count, -1)
    before = (
        present[None, :]
        & (source_dev[None, :] == source_dev[:, None])
        & (members[None, :] < members[:, None])
    )
    slot_at = jnp.sum(before, axis=1)
    recv_row = jnp.where(present, source_dev * slot_cap + slot_at, 0)

    arrived = lax.all_to_all(
        pack_blocks(
            dest_table,
            (queries[0], keys[0], values[0], cotangent[0]),
            seq_size * slot_cap,
            block_len,
        ),
        "seq",
        split_axis=0,
        concat_axis=0,
        tiled=True,
    )
    block_sums = jnp.sum(arrived[:, 1].astype(jnp.float32), axis=1)
    key_sum = jnp.sum(
        jnp.where(present[:, None], block_sums[recv_row], 0.0).reshape(
            groups_here, cluster_cap, head_dim
        ),
        axis=1,
    )
    present_count = jnp.sum(present.reshape(groups_here, cluster_cap).astype(jnp.int32), axis=1)
    outgoing = routed_attention(
        recv_row.reshape(groups_here, cluster_cap).astype(jnp.int32),
        present_count,
        jnp.where(present, members, 0).reshape(groups_here, cluster_cap).astype(jnp.int32),
        arrived,
    )
    outgoing, key_sum = lax.optimization_barrier((outgoing, key_sum))
    dp_size = lax.axis_size("dp")
    received = jnp.stack(
        [key_sum]
        + [
            lax.ppermute(
                key_sum, "dp", [(index, (index + shift) % dp_size) for index in range(dp_size)]
            )
            for shift in range(1, dp_size)
        ]
    )
    dp_index = lax.axis_index("dp")
    summed = received[dp_index % dp_size]
    for source in range(1, dp_size):
        summed = summed + received[(dp_index - source) % dp_size]
    returned = lax.all_to_all(outgoing, "seq", split_axis=0, concat_axis=0, tiled=True)
    centroid_next = decay_rate * centroid_sums + (1.0 - decay_rate) * summed
    finished = unpack_blocks(dest_table, returned, token_count)
    return tuple(item[None] for item in finished) + (centroid_next,)


def solution(mesh):
    in_specs = (
        P("dp", "seq", None),
        P("dp", "seq", None),
        P("dp", "seq", None),
        P("dp", "seq", None),
        P("dp", None, "seq"),
        P("dp", "seq", None),
        P("seq", None),
    )
    out_specs = (
        P("dp", "seq", None),
        P("dp", "seq", None),
        P("dp", "seq", None),
        P("dp", "seq", None),
        P("seq", None),
    )
    return jax.shard_map(
        per_device, mesh=mesh, in_specs=in_specs, out_specs=out_specs, check_vma=False
    )
```

```python
import math

import jax
import jax.numpy as jnp
from jax import lax
from jax.experimental import pallas as pl
from jax.experimental.pallas import tpu as pltpu
from jax.sharding import PartitionSpec as P

decay_rate = 0.99
neg_fill = -1e30


def attend_block(q, k, v, g, query_pos, key_pos):
    score_scale = 1.0 / math.sqrt(q.shape[-1])
    scores = (
        lax.dot_general(q, k, (((1,), (1,)), ((), ())), preferred_element_type=jnp.float32)
        * score_scale
    )
    visible = key_pos <= query_pos
    scores = jnp.where(visible, scores, neg_fill)
    row_max = jnp.max(scores, axis=-1, keepdims=True)
    raised = jnp.exp(scores - row_max)
    probabilities = jnp.where(visible, raised / jnp.sum(raised, axis=-1, keepdims=True), 0.0)
    weights = probabilities.astype(jnp.bfloat16)
    out_full = jnp.dot(weights, v, preferred_element_type=jnp.float32)
    dprobs = lax.dot_general(g, v, (((1,), (1,)), ((), ())), preferred_element_type=jnp.float32)
    row_dot = jnp.sum(g.astype(jnp.float32) * out_full, axis=-1, keepdims=True)
    dscores = (probabilities * (dprobs - row_dot) * score_scale).astype(jnp.bfloat16)
    grad_values = lax.dot_general(
        weights, g, (((0,), (0,)), ((), ())), preferred_element_type=jnp.float32
    )
    grad_queries = jnp.dot(dscores, k, preferred_element_type=jnp.float32)
    grad_keys = lax.dot_general(
        dscores, q, (((0,), (0,)), ((), ())), preferred_element_type=jnp.float32
    )
    return (out_full, grad_queries, grad_keys, grad_values)


def routed_kernel(recv_ref, count_ref, member_ref, arrived_ref, out_ref, sums_ref):
    cluster_count, cluster_cap = member_ref.shape
    block_len = arrived_ref.shape[2]

    sums_ref[...] = jnp.zeros(sums_ref.shape, sums_ref.dtype)

    def one_cluster(cluster, carry):
        present_count = count_ref[cluster]
        for used in range(1, cluster_cap + 1):

            @pl.when(present_count == used)
            def _():
                rows = [recv_ref[cluster, slot] for slot in range(used)]
                tiles = [
                    jnp.concatenate([arrived_ref[row, index] for row in rows], axis=0)
                    for index in range(4)
                ]
                offsets = lax.broadcasted_iota(jnp.int32, (used * block_len, 1), 0)
                query_pos = offsets % block_len
                key_offsets = lax.broadcasted_iota(jnp.int32, (1, used * block_len), 1)
                key_pos = key_offsets % block_len
                for slot in range(used):
                    base = member_ref[cluster, slot] * block_len
                    query_pos = jnp.where(offsets // block_len == slot, query_pos + base, query_pos)
                    key_pos = jnp.where(key_offsets // block_len == slot, key_pos + base, key_pos)
                results = attend_block(*tiles, query_pos, key_pos)
                key_total = jnp.sum(tiles[1].astype(jnp.float32), axis=0, keepdims=True)
                sums_ref[cluster] = jnp.broadcast_to(key_total, sums_ref.shape[1:])
                for slot in range(used):
                    for index in range(4):
                        out_ref[rows[slot], index] = results[index][
                            slot * block_len : (slot + 1) * block_len
                        ].astype(out_ref.dtype)

        return carry

    lax.fori_loop(0, cluster_count, one_cluster, 0, unroll=2)


def routed_attention(recv_table, present_count, member_table, arrived):
    smem = pl.BlockSpec(memory_space=pltpu.SMEM)
    vmem = pl.BlockSpec(memory_space=pltpu.VMEM)
    return pl.pallas_call(
        routed_kernel,
        out_shape=(
            jax.ShapeDtypeStruct(arrived.shape, arrived.dtype),
            jax.ShapeDtypeStruct((member_table.shape[0], 8, arrived.shape[3]), jnp.float32),
        ),
        in_specs=[smem, smem, smem, vmem],
        out_specs=(vmem, vmem),
    )(recv_table, present_count, member_table, arrived)


def pack_kernel(dest_ref, *refs):
    in_refs, out_ref = refs[:-1], refs[-1]
    head_count, block_count = dest_ref.shape
    block_len = out_ref.shape[2]
    head_dim = out_ref.shape[3]
    for head in range(head_count):
        for block in range(block_count):
            slot = dest_ref[head, block]
            for index, in_ref in enumerate(in_refs):
                out_ref[slot, index] = in_ref[
                    block * block_len : (block + 1) * block_len,
                    head * head_dim : (head + 1) * head_dim,
                ]


def unpack_kernel(dest_ref, in_ref, *out_refs):
    head_count, block_count = dest_ref.shape
    block_len = in_ref.shape[2]
    head_dim = in_ref.shape[3]
    for head in range(head_count):
        for block in range(block_count):
            slot = dest_ref[head, block]
            for index, out_ref in enumerate(out_refs):
                out_ref[
                    block * block_len : (block + 1) * block_len,
                    head * head_dim : (head + 1) * head_dim,
                ] = in_ref[slot, index]


def pack_blocks(dest_table, sources, slot_count, block_len):
    smem = pl.BlockSpec(memory_space=pltpu.SMEM)
    vmem = pl.BlockSpec(memory_space=pltpu.VMEM)
    head_dim = sources[0].shape[1] // dest_table.shape[0]
    return pl.pallas_call(
        pack_kernel,
        out_shape=jax.ShapeDtypeStruct(
            (slot_count, len(sources), block_len, head_dim), sources[0].dtype
        ),
        in_specs=[smem] + [vmem] * len(sources),
        out_specs=vmem,
    )(dest_table, *sources)


def unpack_blocks(dest_table, returned, token_count):
    smem = pl.BlockSpec(memory_space=pltpu.SMEM)
    vmem = pl.BlockSpec(memory_space=pltpu.VMEM)
    width = dest_table.shape[0] * returned.shape[3]
    count = returned.shape[1]
    return pl.pallas_call(
        unpack_kernel,
        out_shape=tuple(
            jax.ShapeDtypeStruct((token_count, width), returned.dtype) for _ in range(count)
        ),
        in_specs=[smem, vmem],
        out_specs=tuple(vmem for _ in range(count)),
    )(dest_table, returned)


def per_device(queries, keys, values, cotangent, cluster_of, block_list, centroid_sums):
    seq_size = lax.axis_size("seq")
    head_count = cluster_of.shape[1]
    block_count = cluster_of.shape[2]
    token_count = queries.shape[1]
    block_len = token_count // block_count
    head_dim = centroid_sums.shape[1]
    groups_here = block_list.shape[1]
    cluster_cap = block_list.shape[2]
    owner_count = seq_size // head_count
    slot_cap = min(block_count, max(1, 2 * block_count // owner_count))
    cluster_ids = cluster_of[0]
    owner_local = cluster_ids // groups_here
    earlier = jnp.arange(block_count)[:, None] < jnp.arange(block_count)[None, :]
    same_owner = owner_local[:, :, None] == owner_local[:, None, :]
    slot_of = jnp.sum(same_owner & earlier[None], axis=1)
    dest_table = (
        owner_local * slot_cap + jnp.minimum(slot_of, slot_cap - 1)
    ).astype(jnp.int32) + (jnp.arange(head_count) * owner_count * slot_cap)[:, None].astype(jnp.int32)

    members = block_list[0].reshape(-1)
    present = members >= 0
    source_dev = jnp.where(present, members // block_count, -1)
    before = (
        present[None, :]
        & (source_dev[None, :] == source_dev[:, None])
        & (members[None, :] < members[:, None])
    )
    slot_at = jnp.sum(before, axis=1)
    recv_row = jnp.where(present, source_dev * slot_cap + slot_at, 0)

    arrived = lax.all_to_all(
        pack_blocks(
            dest_table,
            (queries[0], keys[0], values[0], cotangent[0]),
            seq_size * slot_cap,
            block_len,
        ),
        "seq",
        split_axis=0,
        concat_axis=0,
        tiled=True,
    )
    present_count = jnp.sum(present.reshape(groups_here, cluster_cap).astype(jnp.int32), axis=1)
    outgoing, key_sums = routed_attention(
        recv_row.reshape(groups_here, cluster_cap).astype(jnp.int32),
        present_count,
        jnp.where(present, members, 0).reshape(groups_here, cluster_cap).astype(jnp.int32),
        arrived,
    )
    key_sum = key_sums[:, 0]
    dp_size = lax.axis_size("dp")
    received = jnp.stack(
        [key_sum]
        + [
            lax.ppermute(
                key_sum, "dp", [(index, (index + shift) % dp_size) for index in range(dp_size)]
            )
            for shift in range(1, dp_size)
        ]
    )
    dp_index = lax.axis_index("dp")
    summed = received[dp_index % dp_size]
    for source in range(1, dp_size):
        summed = summed + received[(dp_index - source) % dp_size]
    returned = lax.all_to_all(outgoing, "seq", split_axis=0, concat_axis=0, tiled=True)
    centroid_next = decay_rate * centroid_sums + (1.0 - decay_rate) * summed
    finished = unpack_blocks(dest_table, returned, token_count)
    return tuple(item[None] for item in finished) + (centroid_next,)


def solution(mesh):
    in_specs = (
        P("dp", "seq", None),
        P("dp", "seq", None),
        P("dp", "seq", None),
        P("dp", "seq", None),
        P("dp", None, "seq"),
        P("dp", "seq", None),
        P("seq", None),
    )
    out_specs = (
        P("dp", "seq", None),
        P("dp", "seq", None),
        P("dp", "seq", None),
        P("dp", "seq", None),
        P("seq", None),
    )
    return jax.shard_map(
        per_device, mesh=mesh, in_specs=in_specs, out_specs=out_specs, check_vma=False
    )
```

```python
import math

import jax
import jax.numpy as jnp
from jax import lax
from jax.experimental import pallas as pl
from jax.experimental.pallas import tpu as pltpu
from jax.sharding import PartitionSpec as P

decay_rate = 0.99
neg_fill = -1e30


def attend_block(q, k, v, g, query_pos, key_pos):
    score_scale = 1.0 / math.sqrt(q.shape[-1])
    scores = (
        lax.dot_general(q, k, (((1,), (1,)), ((), ())), preferred_element_type=jnp.float32)
        * score_scale
    )
    visible = key_pos <= query_pos
    scores = jnp.where(visible, scores, neg_fill)
    row_max = jnp.max(scores, axis=-1, keepdims=True)
    raised = jnp.exp(scores - row_max)
    probabilities = jnp.where(visible, raised / jnp.sum(raised, axis=-1, keepdims=True), 0.0)
    weights = probabilities.astype(jnp.bfloat16)
    out_full = jnp.dot(weights, v, preferred_element_type=jnp.float32)
    dprobs = lax.dot_general(g, v, (((1,), (1,)), ((), ())), preferred_element_type=jnp.float32)
    row_dot = jnp.sum(g.astype(jnp.float32) * out_full, axis=-1, keepdims=True)
    dscores = (probabilities * (dprobs - row_dot) * score_scale).astype(jnp.bfloat16)
    grad_values = lax.dot_general(
        weights, g, (((0,), (0,)), ((), ())), preferred_element_type=jnp.float32
    )
    grad_queries = jnp.dot(dscores, k, preferred_element_type=jnp.float32)
    grad_keys = lax.dot_general(
        dscores, q, (((0,), (0,)), ((), ())), preferred_element_type=jnp.float32
    )
    return (out_full, grad_queries, grad_keys, grad_values)


def routed_kernel(recv_ref, count_ref, member_ref, arrived_ref, out_ref):
    cluster_count, cluster_cap = member_ref.shape
    block_len = arrived_ref.shape[2]

    def one_cluster(cluster, carry):
        present_count = count_ref[cluster]
        for used in range(1, cluster_cap + 1):

            @pl.when(present_count == used)
            def _():
                rows = [recv_ref[cluster, slot] for slot in range(used)]
                tiles = [
                    jnp.concatenate([arrived_ref[row, index] for row in rows], axis=0)
                    for index in range(4)
                ]
                offsets = lax.broadcasted_iota(jnp.int32, (used * block_len, 1), 0)
                query_pos = offsets % block_len
                key_offsets = lax.broadcasted_iota(jnp.int32, (1, used * block_len), 1)
                key_pos = key_offsets % block_len
                for slot in range(used):
                    base = member_ref[cluster, slot] * block_len
                    query_pos = jnp.where(offsets // block_len == slot, query_pos + base, query_pos)
                    key_pos = jnp.where(key_offsets // block_len == slot, key_pos + base, key_pos)
                results = attend_block(*tiles, query_pos, key_pos)
                for slot in range(used):
                    for index in range(4):
                        out_ref[rows[slot], index] = results[index][
                            slot * block_len : (slot + 1) * block_len
                        ].astype(out_ref.dtype)

        return carry

    lax.fori_loop(0, cluster_count, one_cluster, 0, unroll=2)


def routed_attention(recv_table, present_count, member_table, arrived):
    smem = pl.BlockSpec(memory_space=pltpu.SMEM)
    vmem = pl.BlockSpec(memory_space=pltpu.VMEM)
    return pl.pallas_call(
        routed_kernel,
        out_shape=jax.ShapeDtypeStruct(arrived.shape, arrived.dtype),
        in_specs=[smem, smem, smem, vmem],
        out_specs=vmem,
    )(recv_table, present_count, member_table, arrived)


def pack_kernel(dest_ref, *refs):
    in_refs, out_ref = refs[:-1], refs[-1]
    head_count, block_count = dest_ref.shape
    block_len = out_ref.shape[2]
    head_dim = out_ref.shape[3]
    for head in range(head_count):
        for block in range(block_count):
            slot = dest_ref[head, block]
            for index, in_ref in enumerate(in_refs):
                out_ref[slot, index] = in_ref[
                    block * block_len : (block + 1) * block_len,
                    head * head_dim : (head + 1) * head_dim,
                ]


def unpack_kernel(dest_ref, in_ref, *out_refs):
    head_count, block_count = dest_ref.shape
    block_len = in_ref.shape[2]
    head_dim = in_ref.shape[3]
    for head in range(head_count):
        for block in range(block_count):
            slot = dest_ref[head, block]
            for index, out_ref in enumerate(out_refs):
                out_ref[
                    block * block_len : (block + 1) * block_len,
                    head * head_dim : (head + 1) * head_dim,
                ] = in_ref[slot, index]


def pack_blocks(dest_table, sources, slot_count, block_len):
    smem = pl.BlockSpec(memory_space=pltpu.SMEM)
    vmem = pl.BlockSpec(memory_space=pltpu.VMEM)
    head_dim = sources[0].shape[1] // dest_table.shape[0]
    return pl.pallas_call(
        pack_kernel,
        out_shape=jax.ShapeDtypeStruct(
            (slot_count, len(sources), block_len, head_dim), sources[0].dtype
        ),
        in_specs=[smem] + [vmem] * len(sources),
        out_specs=vmem,
    )(dest_table, *sources)


def unpack_blocks(dest_table, returned, token_count):
    smem = pl.BlockSpec(memory_space=pltpu.SMEM)
    vmem = pl.BlockSpec(memory_space=pltpu.VMEM)
    width = dest_table.shape[0] * returned.shape[3]
    count = returned.shape[1]
    return pl.pallas_call(
        unpack_kernel,
        out_shape=tuple(
            jax.ShapeDtypeStruct((token_count, width), returned.dtype) for _ in range(count)
        ),
        in_specs=[smem, vmem],
        out_specs=tuple(vmem for _ in range(count)),
    )(dest_table, returned)


def per_device(queries, keys, values, cotangent, cluster_of, block_list, centroid_sums):
    seq_size = lax.axis_size("seq")
    head_count = cluster_of.shape[1]
    block_count = cluster_of.shape[2]
    token_count = queries.shape[1]
    block_len = token_count // block_count
    head_dim = centroid_sums.shape[1]
    groups_here = block_list.shape[1]
    cluster_cap = block_list.shape[2]
    owner_count = seq_size // head_count
    slot_cap = min(block_count, max(1, 2 * block_count // owner_count))
    cluster_ids = cluster_of[0]
    owner_local = cluster_ids // groups_here
    earlier = jnp.arange(block_count)[:, None] < jnp.arange(block_count)[None, :]
    same_owner = owner_local[:, :, None] == owner_local[:, None, :]
    slot_of = jnp.sum(same_owner & earlier[None], axis=1)
    dest_table = (
        owner_local * slot_cap + jnp.minimum(slot_of, slot_cap - 1)
    ).astype(jnp.int32) + (jnp.arange(head_count) * owner_count * slot_cap)[:, None].astype(jnp.int32)

    members = block_list[0].reshape(-1)
    present = members >= 0
    source_dev = jnp.where(present, members // block_count, -1)
    before = (
        present[None, :]
        & (source_dev[None, :] == source_dev[:, None])
        & (members[None, :] < members[:, None])
    )
    slot_at = jnp.sum(before, axis=1)
    recv_row = jnp.where(present, source_dev * slot_cap + slot_at, 0)

    arrived = lax.all_to_all(
        pack_blocks(
            dest_table,
            (queries[0], keys[0], values[0], cotangent[0]),
            seq_size * slot_cap,
            block_len,
        ),
        "seq",
        split_axis=0,
        concat_axis=0,
        tiled=True,
    )
    block_sums = jnp.sum(arrived[:, 1].astype(jnp.float32), axis=1)
    key_sum = jnp.sum(
        jnp.where(present[:, None], block_sums[recv_row], 0.0).reshape(
            groups_here, cluster_cap, head_dim
        ),
        axis=1,
    )
    present_count = jnp.sum(present.reshape(groups_here, cluster_cap).astype(jnp.int32), axis=1)
    outgoing = routed_attention(
        recv_row.reshape(groups_here, cluster_cap).astype(jnp.int32),
        present_count,
        jnp.where(present, members, 0).reshape(groups_here, cluster_cap).astype(jnp.int32),
        arrived,
    )
    outgoing, key_sum = lax.optimization_barrier((outgoing, key_sum))
    dp_size = lax.axis_size("dp")
    summed = key_sum
    stride = 1
    while stride < dp_size:
        summed = summed + lax.ppermute(
            summed, "dp", [(index, index ^ stride) for index in range(dp_size)]
        )
        stride *= 2
    returned = lax.all_to_all(outgoing, "seq", split_axis=0, concat_axis=0, tiled=True)
    centroid_next = decay_rate * centroid_sums + (1.0 - decay_rate) * summed
    finished = unpack_blocks(dest_table, returned, token_count)
    return tuple(item[None] for item in finished) + (centroid_next,)


def solution(mesh):
    in_specs = (
        P("dp", "seq", None),
        P("dp", "seq", None),
        P("dp", "seq", None),
        P("dp", "seq", None),
        P("dp", None, "seq"),
        P("dp", "seq", None),
        P("seq", None),
    )
    out_specs = (
        P("dp", "seq", None),
        P("dp", "seq", None),
        P("dp", "seq", None),
        P("dp", "seq", None),
        P("seq", None),
    )
    return jax.shard_map(
        per_device, mesh=mesh, in_specs=in_specs, out_specs=out_specs, check_vma=False
    )
```
